128 devices in a mesh: tm: 128 (over x, y, z, core).
Axes of the slice: x: 4, y: 4, z: 4, core: 2. Of those that a mesh axis runs over, the one named last changes fastest.
Arguments:
- observations: float32 [4096, 4, 64], P('tm'), may hold values from -6 to 6
- decay: float32 [4096, 128], P('tm'), may hold values from 0 to 1
- transition: float32 [128, 128], replicated, may hold values from -1 to 1
- obs_map: float32 [64, 128], replicated, may hold values from -0.0625 to 0.0625
- noise_precision: float32 [64], replicated, may hold values from 0.01 to 0.2
- smoother_gain: float32 [128, 128], replicated, may hold values from -1 to 1
Outputs:
- filtered: float32 [4096, 4, 128], P('tm')
- smoothed: float32 [4096, 4, 128], P('tm')
The draws below stay inside these ranges and needn't reach their ends.
All inputs are finite; a program needn't handle non-finite values.
Results may differ from the reference program's by a relative error of at most 0.0003.
Values sent between devices are 32-bit elements; how exact they have to be, the bound alone decides.
No kernel may reach another device: no remote copies, remote signals or barrier semaphores. Data moves between devices by JAX's collectives and lax.ppermute only.
A program may use at most 128 MiB of HBM per device.

```python
import math
import jax
import jax.numpy as jnp
import numpy as np
from jax import lax

S = 128
M = 64
SEQS = 4
TOTAL_EPOCHS = 4096


def butterfly(key):
    matrix = jnp.eye(S, dtype=jnp.float32)
    indices = np.arange(S)
    for level in range(S.bit_length() - 1):
        partner = indices ^ 1 << level
        lower = np.minimum(indices, partner)
        signs = np.where(indices < partner, -1.0, 1.0).astype(np.float32)
        angles = jax.random.uniform(jax.random.fold_in(key, level), (S,), jnp.float32, -math.pi, math.pi)
        paired = angles[lower]
        cosine = jnp.cos(paired)[:, None]
        sine = (jnp.sin(paired) * signs)[:, None]
        matrix = cosine * matrix + sine * matrix[partner]
    return matrix


def draw_transition(key, part):
    return butterfly(jax.random.fold_in(key, 11))


def draw_smoother_gain(key, part):
    return butterfly(jax.random.fold_in(key, 23))


def draw_decay(key, part):
    share = 1.0 / 16.0
    fast = jax.random.uniform(jax.random.fold_in(key, 31), (S,), jnp.float32) < share
    slow_rate = jnp.exp(jax.random.uniform(jax.random.fold_in(key, 32), (S,), jnp.float32, math.log(0.2 / TOTAL_EPOCHS), math.log(1.0 / TOTAL_EPOCHS)))
    fast_rate = jax.random.uniform(jax.random.fold_in(key, 33), (S,), jnp.float32, 1.0 / 50.0, 1.0 / 30.0)
    acquisition_frequency = jnp.where(fast, fast_rate, slow_rate)
    random_perturbation = jnp.exp(jax.random.uniform(jax.random.fold_in(key, 34), (TOTAL_EPOCHS, S), jnp.float32, math.log(0.5), math.log(2.0)))
    spike_present = jax.random.uniform(jax.random.fold_in(key, 35), (TOTAL_EPOCHS, 1), jnp.float32) < 6.0 / TOTAL_EPOCHS
    waveform_amplitude = jax.random.uniform(jax.random.fold_in(key, 36), (TOTAL_EPOCHS, 1), jnp.float32, 0.5, 0.8)
    spike_occurrence = jnp.where(spike_present, waveform_amplitude, 1.0)
    return jnp.exp(-acquisition_frequency[None, :] * random_perturbation) * spike_occurrence


def block_levels(own_key, shape, cuts, least, high):
    level = 1.0
    for axis_at, blocks in cuts:
        draws = jax.random.uniform(jax.random.fold_in(jax.random.fold_in(own_key, 6), axis_at), (blocks,), jnp.float32, least / len(cuts), high / len(cuts))
        level = level * jnp.repeat(jnp.exp(draws), shape[axis_at] // blocks).reshape((-1,) + (1,) * (len(shape) - 1 - axis_at))
    return level


def noise(stream_key, shape, spread, reach, pieces=(), kind=jnp.bfloat16):
    entries = jax.random.normal(stream_key, shape, jnp.float32) * spread
    if len(pieces) > 0:
        entries = block_levels(stream_key, shape, pieces, -0.22, 0.18) * entries
    return jnp.clip(entries, min=-reach, max=reach).astype(kind)


def setup_inputs(seed: int = 0) -> dict:
    arg_keys = jax.random.split(jax.random.key(seed), 7)
    observations = noise(arg_keys[0], (TOTAL_EPOCHS, SEQS, M), 1.0, 6.0, ((0, 128),), jnp.float32)
    decay = draw_decay(jax.random.fold_in(arg_keys[6], 71), 0)
    transition = draw_transition(jax.random.fold_in(arg_keys[6], 71), 0)
    obs_map = noise(arg_keys[3], (M, S), (64 * S) ** -0.5, 0.0625, (), jnp.float32)
    noise_precision = jnp.clip(jnp.exp(jax.random.uniform(arg_keys[4], (M,), jnp.float32, math.log(0.01), math.log(0.2))), 0.01, 0.2)
    smoother_gain = draw_smoother_gain(jax.random.fold_in(arg_keys[6], 71), 0)
    return dict(observations=observations, decay=decay, transition=transition, obs_map=obs_map, noise_precision=noise_precision, smoother_gain=smoother_gain)


def reference(observations, decay, transition, obs_map, noise_precision, smoother_gain):
    highest_level = lax.Precision.HIGHEST
    gain_row_block = obs_map * noise_precision[:, None]
    closed_rows = transition.T - jnp.dot(transition.T, jnp.dot(obs_map.T, gain_row_block, precision=highest_level), precision=highest_level)

    def forward(state, item):
        retain, measured = item
        state = jnp.dot(state * retain, closed_rows, precision=highest_level) + jnp.dot(measured, gain_row_block, precision=highest_level)
        return state, state

    start = jnp.zeros((SEQS, S), jnp.float32)
    _, filtered = lax.scan(forward, start, (decay, observations))
    attenuation_upcoming = jnp.concatenate([decay[1:], jnp.zeros((1, S), jnp.float32)], 0)

    def backward(state, item):
        current, retain = item
        predicted = jnp.dot(current * retain, transition.T, precision=highest_level)
        state = current + jnp.dot((state - predicted) * retain, smoother_gain.T, precision=highest_level)
        return state, state

    _, smoothed = lax.scan(backward, start, (filtered, attenuation_upcoming), reverse=True)
    return filtered, smoothed
```

```python
import jax
import jax.numpy as jnp
from jax import lax
from jax.sharding import PartitionSpec as P

HIGHEST = lax.Precision.HIGHEST


def shifted(x, by):
    count = lax.axis_size("tm")
    pairs = [(i, i + by) for i in range(count) if 0 <= i + by < count]
    return lax.ppermute(x, "tm", pairs)


def inclusive(maps, adds):
    stride = 1
    while stride < maps.shape[0]:
        new_adds = (
            jnp.einsum("tbj,tjk->tbk", adds[:-stride], maps[stride:], precision=HIGHEST)
            + adds[stride:]
        )
        new_maps = jnp.einsum("tij,tjk->tik", maps[:-stride], maps[stride:], precision=HIGHEST)
        maps = jnp.concatenate([maps[:stride], new_maps], 0)
        adds = jnp.concatenate([adds[:stride], new_adds], 0)
        stride *= 2
    return maps, adds


def across(total_map, total_add, direction, fused):
    count = lax.axis_size("tm")
    position = lax.axis_index("tm")
    size = total_map.shape[0]
    stacked_map = jnp.concatenate([total_map, jnp.eye(size, dtype=jnp.float32)], 1)
    stacked_add = jnp.concatenate([total_add, jnp.zeros_like(total_add)], 1)
    span = 1
    while span < count:
        if direction > 0:
            valid = position >= span
        else:
            valid = position + span < count
        if span * 2 >= count:
            got_add = shifted(stacked_add[:, :size], direction * span)
            result = (
                jnp.dot(got_add, stacked_map[:, size:], precision=HIGHEST)
                + stacked_add[:, size:]
            )
            return jnp.where(valid, result, stacked_add[:, size:])
        if fused:
            both = shifted(
                jnp.concatenate([stacked_map[:, :size], stacked_add[:, :size]], 0),
                direction * span,
            )
            got_map, got_add = both[:size], both[size:]
        else:
            got_map = shifted(stacked_map[:, :size], direction * span)
            got_add = shifted(stacked_add[:, :size], direction * span)
        new_map = jnp.dot(got_map, stacked_map, precision=HIGHEST)
        new_add = jnp.dot(got_add, stacked_map, precision=HIGHEST) + stacked_add
        stacked_map = jnp.where(valid, new_map, stacked_map)
        stacked_add = jnp.where(valid, new_add, stacked_add)
        span *= 2
    return stacked_add[:, size:]


def local(observations, decay, transition, obs_map, noise_precision, smoother_gain):
    gain_rows = obs_map * noise_precision[:, None]
    closed_rows = transition.T - jnp.dot(
        transition.T,
        jnp.dot(obs_map.T, gain_rows, precision=HIGHEST),
        precision=HIGHEST,
    )
    forward_maps = decay[:, :, None] * closed_rows[None]
    forward_adds = jnp.einsum("wyn,nx->wyx", observations, gain_rows, precision=HIGHEST)
    prefix_maps, prefix_adds = inclusive(forward_maps, forward_adds)
    entering = across(prefix_maps[-1], prefix_adds[-1], 1, True)
    filtered = (
        jnp.einsum("bs,tsr->tbr", entering, prefix_maps, precision=HIGHEST) + prefix_adds
    )

    following = shifted(decay[:1], -1)
    upcoming = jnp.concatenate([decay[1:], following], 0)
    backward_maps = upcoming[:, :, None] * smoother_gain.T[None]
    predicted = jnp.einsum(
        "tbs,sr->tbr", filtered * upcoming[:, None, :], transition.T, precision=HIGHEST
    )
    backward_adds = filtered - jnp.einsum(
        "tbs,sr->tbr", predicted * upcoming[:, None, :], smoother_gain.T, precision=HIGHEST
    )
    reverse_maps, reverse_adds = inclusive(backward_maps[::-1], backward_adds[::-1])
    arriving = across(reverse_maps[-1], reverse_adds[-1], -1, False)
    smoothed = (
        jnp.einsum("bs,tsr->tbr", arriving, reverse_maps, precision=HIGHEST) + reverse_adds
    )[::-1]
    return filtered, smoothed


def solution(mesh):
    in_specs = (P("tm", None, None), P("tm", None), P(), P(), P(), P())
    out_specs = (P("tm", None, None), P("tm", None, None))
    return jax.shard_map(local, mesh=mesh, in_specs=in_specs, out_specs=out_specs, check_vma=False)
```

```python
import jax
import jax.numpy as jnp
from jax import lax
from jax.sharding import PartitionSpec as P

HIGHEST = lax.Precision.HIGHEST


def dot(a, b):
    return jnp.dot(a, b, precision=HIGHEST)


def shifted(x, by):
    count = lax.axis_size("tm")
    pairs = [(i, i + by) for i in range(count) if 0 <= i + by < count]
    return lax.ppermute(x, "tm", pairs)


def up_sweep(maps, adds):
    levels = [(maps, adds)]
    while maps.shape[0] > 1:
        pairs = maps.reshape((-1, 2) + maps.shape[1:])
        if adds is not None:
            halves = adds.reshape((-1, 2) + adds.shape[1:])
            adds = (
                jnp.einsum("tbj,tjk->tbk", halves[:, 0], pairs[:, 1], precision=HIGHEST)
                + halves[:, 1]
            )
        maps = jnp.einsum("tij,tjk->tik", pairs[:, 0], pairs[:, 1], precision=HIGHEST)
        levels.append((maps, adds))
    return levels


def down_sweep_maps(levels):
    size = levels[0][0].shape[-1]
    excl = None
    for maps, _ in reversed(levels[:-1]):
        left = maps.reshape((-1, 2) + maps.shape[1:])[:, 0]
        if excl is None:
            excl = jnp.eye(size, dtype=jnp.float32)[None]
            odd = left
        else:
            odd = jnp.einsum("tij,tjk->tik", excl, left, precision=HIGHEST)
        excl = jnp.stack([excl, odd], 1).reshape((-1,) + maps.shape[1:])
    return excl


def down_sweep_adds(levels, adds_levels):
    excl = None
    for (maps, _), adds in zip(reversed(levels[:-1]), reversed(adds_levels[:-1])):
        left_map = maps.reshape((-1, 2) + maps.shape[1:])[:, 0]
        left_add = adds.reshape((-1, 2) + adds.shape[1:])[:, 0]
        if excl is None:
            excl = jnp.zeros_like(left_add[:1])
            odd = left_add
        else:
            odd = jnp.einsum("tbj,tjk->tbk", excl, left_map, precision=HIGHEST) + left_add
        excl = jnp.stack([excl, odd], 1).reshape((-1,) + adds.shape[1:])
    return excl


def up_sweep_adds(levels, adds):
    out = [adds]
    for maps, _ in levels[:-1]:
        pairs = maps.reshape((-1, 2) + maps.shape[1:])
        halves = adds.reshape((-1, 2) + adds.shape[1:])
        adds = (
            jnp.einsum("tbj,tjk->tbk", halves[:, 0], pairs[:, 1], precision=HIGHEST)
            + halves[:, 1]
        )
        out.append(adds)
    return out


class Chain:
    def __init__(self, mode, store, size, rows):
        self.mode, self.store, self.size, self.rows = mode, store, size, rows
        self.taken = 0

    def identity(self):
        eye = jnp.eye(self.size, dtype=jnp.float32)
        zero = jnp.zeros((self.rows, self.size), jnp.float32)
        return (eye if self.mode != "adds" else None, zero if self.mode != "maps" else None)

    def compose(self, a, b):
        if a is None:
            return b
        if b is None:
            return a
        if self.mode == "full":
            return (dot(a[0], b[0]), dot(a[1], b[0]) + b[1])
        if self.mode == "maps":
            self.store.append(b[0])
            return (dot(a[0], b[0]), None)
        right = self.store[self.taken]
        self.taken += 1
        return (None, dot(a[1], right) + b[1])

    def pick(self, options, index):
        ident = self.identity()
        options = [ident if o is None else o for o in options]
        parts = []
        for k in range(2):
            if options[0][k] is None:
                parts.append(None)
            else:
                stacked = jnp.stack([o[k] for o in options])
                parts.append(lax.dynamic_index_in_dim(stacked, index, 0, keepdims=False))
        return tuple(parts)


def levels_of(count):
    levels = []
    stride = 1
    while stride < count:
        size = 2 if stride == 1 or (count // stride) % 4 != 0 else 4
        levels.append((stride, size))
        stride *= size
    return levels


def group_gather(x, stride, size):
    count = lax.axis_size("tm")
    position = (lax.axis_index("tm") // stride) % size
    relative = [x]
    for r in range(1, size):
        pairs = []
        for dst in range(count):
            q = (dst // stride) % size
            pairs.append((dst + (((q + r) % size) - q) * stride, dst))
        relative.append(lax.ppermute(x, "tm", pairs))
    stacked = jnp.stack(relative)
    return [
        lax.dynamic_index_in_dim(stacked, (m - position) % size, 0, keepdims=False)
        for m in range(size)
    ]


def level_step(chain, items, before, position, size, reverse, want_total):
    if reverse:
        items = items[::-1]
        position = size - 1 - position
    prefixes = [None, items[0]]
    if size == 2:
        total = chain.compose(items[0], items[1]) if want_total else None
    else:
        first_two = chain.compose(items[0], items[1])
        prefixes.append(first_two)
        prefixes.append(chain.compose(first_two, items[2]))
        total = (
            chain.compose(first_two, chain.compose(items[2], items[3])) if want_total else None
        )
    chosen = chain.pick(prefixes[:size], position)
    return total, chain.compose(chosen, before)


def local(observations, decay, transition, obs_map, noise_precision, smoother_gain):
    size = transition.shape[0]
    rows = observations.shape[1]
    count = lax.axis_size("tm")
    index = lax.axis_index("tm")
    gain_rows = obs_map * noise_precision[:, None]
    closed_rows = transition.T - dot(transition.T, dot(obs_map.T, gain_rows))
    forward_maps = decay[:, :, None] * closed_rows[None]
    forward_adds = jnp.einsum("wyn,nx->wyx", observations, gain_rows, precision=HIGHEST)

    following = shifted(decay[:1], -1)
    upcoming = jnp.concatenate([decay[1:], following], 0)
    backward_maps = (upcoming[:, :, None] * smoother_gain.T[None])[::-1]

    forward_tree = up_sweep(forward_maps, forward_adds)
    backward_tree = up_sweep(backward_maps, None)
    block_map, block_add = forward_tree[-1][0][0], forward_tree[-1][1][0]
    back_map = backward_tree[-1][0][0]

    levels = levels_of(count)
    full = Chain("full", None, size, rows)
    maps_only = Chain("maps", [], size, rows)
    total_f, before_f = (block_map, block_add), None
    total_b, before_b = (back_map, None), None
    late = forward_tree
    for depth, (stride, group) in enumerate(levels):
        last = depth == len(levels) - 1
        message = jnp.concatenate([total_f[0], total_f[1], total_b[0]], 0)
        members = group_gather(message, stride, group)
        if depth == 0:
            late, members = lax.optimization_barrier((late, members))
        position = (index // stride) % group
        items_f = [(m[:size], m[size:size + rows]) for m in members]
        items_b = [(m[size + rows:], None) for m in members]
        total_f, before_f = level_step(full, items_f, before_f, position, group, False, not last)
        total_b, before_b = level_step(maps_only, items_b, before_b, position, group, True, not last)
    entering = before_f[1]

    excl_maps = down_sweep_maps(late)
    excl_adds = down_sweep_adds(late, [a for _, a in late])
    previous = jnp.einsum("bs,tsr->tbr", entering, excl_maps, precision=HIGHEST) + excl_adds
    filtered = (
        jnp.einsum("tbs,sr->tbr", previous * decay[:, None, :], closed_rows, precision=HIGHEST)
        + forward_adds
    )
    predicted = jnp.einsum(
        "tbs,sr->tbr", filtered * upcoming[:, None, :], transition.T, precision=HIGHEST
    )
    backward_adds = filtered - jnp.einsum(
        "tbs,sr->tbr", predicted * upcoming[:, None, :], smoother_gain.T, precision=HIGHEST
    )
    back_adds = up_sweep_adds(backward_tree, backward_adds[::-1])

    adds_only = Chain("adds", maps_only.store, size, rows)
    total_b, before_b = (None, back_adds[-1][0]), None
    late_b = (backward_tree, back_adds)
    for depth, (stride, group) in enumerate(levels):
        last = depth == len(levels) - 1
        members = group_gather(total_b[1], stride, group)
        if depth == 0:
            late_b, members = lax.optimization_barrier((late_b, members))
        position = (index // stride) % group
        items_b = [(None, m) for m in members]
        total_b, before_b = level_step(adds_only, items_b, before_b, position, group, True, not last)
    arriving = before_b[1]
    back_excl_maps = down_sweep_maps(late_b[0])
    back_excl_adds = down_sweep_adds(late_b[0], late_b[1])
    following_state = (
        jnp.einsum("bs,tsr->tbr", arriving, back_excl_maps, precision=HIGHEST) + back_excl_adds
    )[::-1]
    smoothed = (
        jnp.einsum(
            "tbs,sr->tbr", following_state * upcoming[:, None, :], smoother_gain.T, precision=HIGHEST
        )
        + backward_adds
    )
    return filtered, smoothed


def solution(mesh):
    in_specs = (P("tm", None, None), P("tm", None), P(), P(), P(), P())
    out_specs = (P("tm", None, None), P("tm", None, None))
    return jax.shard_map(local, mesh=mesh, in_specs=in_specs, out_specs=out_specs, check_vma=False)
```

```python
import jax
import jax.numpy as jnp
from jax import lax
from jax.sharding import PartitionSpec as P

HIGHEST = lax.Precision.HIGHEST


def dot(a, b):
    return jnp.dot(a, b, precision=HIGHEST)


def shifted(x, by):
    count = lax.axis_size("tm")
    pairs = [(i, i + by) for i in range(count) if 0 <= i + by < count]
    return lax.ppermute(x, "tm", pairs)


def up_sweep(maps, adds):
    levels = [(maps, adds)]
    while maps.shape[0] > 1:
        pairs = maps.reshape((-1, 2) + maps.shape[1:])
        if adds is not None:
            halves = adds.reshape((-1, 2) + adds.shape[1:])
            adds = (
                jnp.einsum("tbj,tjk->tbk", halves[:, 0], pairs[:, 1], precision=HIGHEST)
                + halves[:, 1]
            )
        maps = jnp.einsum("tij,tjk->tik", pairs[:, 0], pairs[:, 1], precision=HIGHEST)
        levels.append((maps, adds))
    return levels


def down_sweep_maps(levels):
    size = levels[0][0].shape[-1]
    excl = None
    for maps, _ in reversed(levels[:-1]):
        left = maps.reshape((-1, 2) + maps.shape[1:])[:, 0]
        if excl is None:
            excl = jnp.eye(size, dtype=jnp.float32)[None]
            odd = left
        else:
            odd = jnp.einsum("tij,tjk->tik", excl, left, precision=HIGHEST)
        excl = jnp.stack([excl, odd], 1).reshape((-1,) + maps.shape[1:])
    return excl


def down_sweep_adds(levels, adds_levels):
    excl = None
    for (maps, _), adds in zip(reversed(levels[:-1]), reversed(adds_levels[:-1])):
        left_map = maps.reshape((-1, 2) + maps.shape[1:])[:, 0]
        left_add = adds.reshape((-1, 2) + adds.shape[1:])[:, 0]
        if excl is None:
            excl = jnp.zeros_like(left_add[:1])
            odd = left_add
        else:
            odd = jnp.einsum("tbj,tjk->tbk", excl, left_map, precision=HIGHEST) + left_add
        excl = jnp.stack([excl, odd], 1).reshape((-1,) + adds.shape[1:])
    return excl


def up_sweep_adds(levels, adds):
    out = [adds]
    for maps, _ in levels[:-1]:
        pairs = maps.reshape((-1, 2) + maps.shape[1:])
        halves = adds.reshape((-1, 2) + adds.shape[1:])
        adds = (
            jnp.einsum("tbj,tjk->tbk", halves[:, 0], pairs[:, 1], precision=HIGHEST)
            + halves[:, 1]
        )
        out.append(adds)
    return out


def exchanged(x, bit):
    count = lax.axis_size("tm")
    return lax.ppermute(x, "tm", [(i, i ^ bit) for i in range(count)])


def batched(lhs, rhs):
    return jnp.einsum("kij,kjl->kil", jnp.stack(lhs), jnp.stack(rhs), precision=HIGHEST)


def local(observations, decay, transition, obs_map, noise_precision, smoother_gain):
    size = transition.shape[0]
    count = lax.axis_size("tm")
    index = lax.axis_index("tm")
    gain_rows = obs_map * noise_precision[:, None]
    closed_rows = transition.T - dot(transition.T, dot(obs_map.T, gain_rows))
    forward_adds = jnp.einsum("wyn,nx->wyx", observations, gain_rows, precision=HIGHEST)

    following = shifted(decay[:1], -1)
    upcoming = jnp.concatenate([decay[1:], following], 0)
    step_maps = jnp.stack([decay, upcoming[::-1]])[:, :, :, None] * jnp.stack(
        [closed_rows, smoother_gain.T]
    )[:, None]

    tree = [(step_maps, forward_adds)]
    maps, adds = step_maps, forward_adds
    while maps.shape[1] > 1:
        pairs = maps.reshape((2, -1, 2) + maps.shape[2:])
        halves = adds.reshape((-1, 2) + adds.shape[1:])
        adds = (
            jnp.einsum("tbj,tjk->tbk", halves[:, 0], pairs[0, :, 1], precision=HIGHEST)
            + halves[:, 1]
        )
        maps = jnp.einsum("dtij,dtjk->dtik", pairs[:, :, 0], pairs[:, :, 1], precision=HIGHEST)
        tree.append((maps, adds))
    forward_tree = [(m[0], a) for m, a in tree]
    backward_tree = [(m[1], None) for m, _ in tree]

    rounds = []
    bit = 1
    while bit < count:
        rounds.append(bit)
        bit *= 2
    eye = jnp.eye(size, dtype=jnp.float32)
    total_map, total_add, before_map, before_add = maps[0, 0], adds[0], eye, jnp.zeros_like(adds[0])
    back_total, back_before = maps[1, 0], eye
    stored = []
    late = forward_tree
    for k, bit in enumerate(rounds):
        upper = (index & bit) != 0
        if k == len(rounds) - 1:
            got_add = exchanged(total_add, bit)
            entering = jnp.where(upper, dot(got_add, before_map) + before_add, before_add)
            stored.append((back_total, back_total, back_before))
            break
        message = jnp.concatenate([total_map, total_add, back_total], 0)
        got = exchanged(message, bit)
        if k == 0:
            late, got = lax.optimization_barrier((late, got))
        got_map, got_add, got_back = got[:size], got[size:-size], got[-size:]
        first_map = jnp.where(upper, got_map, total_map)
        second_map = jnp.where(upper, total_map, got_map)
        first_add = jnp.where(upper, got_add, total_add)
        second_add = jnp.where(upper, total_add, got_add)
        back_first = jnp.where(upper, back_total, got_back)
        back_second = jnp.where(upper, got_back, back_total)
        stored.append((back_total, back_second, back_before))
        products = batched(
            [first_map, got_map, back_first, got_back],
            [second_map, before_map, back_second, back_before],
        )
        offsets = batched([first_add, got_add], [second_map, before_map])
        total_map, total_add = products[0], offsets[0] + second_add
        before_map = jnp.where(upper, products[1], before_map)
        before_add = jnp.where(upper, offsets[1] + before_add, before_add)
        back_total = products[2]
        back_before = jnp.where(upper, back_before, products[3])

    excl_maps = down_sweep_maps(late)
    excl_adds = down_sweep_adds(late, [a for _, a in late])
    previous = jnp.einsum("bs,tsr->tbr", entering, excl_maps, precision=HIGHEST) + excl_adds
    filtered = (
        jnp.einsum("tbs,sr->tbr", previous * decay[:, None, :], closed_rows, precision=HIGHEST)
        + forward_adds
    )
    predicted = jnp.einsum(
        "tbs,sr->tbr", filtered * upcoming[:, None, :], transition.T, precision=HIGHEST
    )
    backward_adds = filtered - jnp.einsum(
        "tbs,sr->tbr", predicted * upcoming[:, None, :], smoother_gain.T, precision=HIGHEST
    )
    back_adds = up_sweep_adds(backward_tree, backward_adds[::-1])

    total_add = back_adds[-1][0]
    before_add = jnp.zeros_like(total_add)
    late_b = (backward_tree, back_adds)
    for k, bit in enumerate(rounds):
        upper = (index & bit) != 0
        own_map, second_map, own_before = stored[k]
        got_add = exchanged(total_add, bit)
        if k == 0:
            late_b, got_add = lax.optimization_barrier((late_b, got_add))
        if k == len(rounds) - 1:
            before_add = jnp.where(upper, before_add, dot(got_add, own_before) + before_add)
            break
        first_add = jnp.where(upper, total_add, got_add)
        second_add = jnp.where(upper, got_add, total_add)
        offsets = batched([first_add, got_add], [second_map, own_before])
        total_add = offsets[0] + second_add
        before_add = jnp.where(upper, before_add, offsets[1] + before_add)
    arriving = before_add
    back_excl_maps = down_sweep_maps(late_b[0])
    back_excl_adds = down_sweep_adds(late_b[0], late_b[1])
    following_state = (
        jnp.einsum("bs,tsr->tbr", arriving, back_excl_maps, precision=HIGHEST) + back_excl_adds
    )[::-1]
    smoothed = (
        jnp.einsum(
            "tbs,sr->tbr", following_state * upcoming[:, None, :], smoother_gain.T, precision=HIGHEST
        )
        + backward_adds
    )
    return filtered, smoothed


def solution(mesh):
    in_specs = (P("tm", None, None), P("tm", None), P(), P(), P(), P())
    out_specs = (P("tm", None, None), P("tm", None, None))
    return jax.shard_map(local, mesh=mesh, in_specs=in_specs, out_specs=out_specs, check_vma=False)
```

```python
import jax
import jax.numpy as jnp
from jax import lax
from jax.sharding import PartitionSpec as P

PRECISION = lax.Precision.HIGHEST


def dot(a, b):
    return jnp.dot(a, b, precision=PRECISION)


def shifted(x, by):
    count = lax.axis_size("tm")
    pairs = [(i, i + by) for i in range(count) if 0 <= i + by < count]
    return lax.ppermute(x, "tm", pairs)


def up_sweep(maps, adds):
    levels = [(maps, adds)]
    while maps.shape[0] > 1:
        pairs = maps.reshape((-1, 2) + maps.shape[1:])
        if adds is not None:
            halves = adds.reshape((-1, 2) + adds.shape[1:])
            adds = (
                jnp.einsum("tbj,tjk->tbk", halves[:, 0], pairs[:, 1], precision=PRECISION)
                + halves[:, 1]
            )
        maps = jnp.einsum("tij,tjk->tik", pairs[:, 0], pairs[:, 1], precision=PRECISION)
        levels.append((maps, adds))
    return levels


def down_sweep_maps(levels):
    size = levels[0][0].shape[-1]
    excl = None
    for maps, _ in reversed(levels[:-1]):
        left = maps.reshape((-1, 2) + maps.shape[1:])[:, 0]
        if excl is None:
            excl = jnp.eye(size, dtype=jnp.float32)[None]
            odd = left
        else:
            odd = jnp.einsum("tij,tjk->tik", excl, left, precision=PRECISION)
        excl = jnp.stack([excl, odd], 1).reshape((-1,) + maps.shape[1:])
    return excl


def down_sweep_adds(levels, adds_levels):
    excl = None
    for (maps, _), adds in zip(reversed(levels[:-1]), reversed(adds_levels[:-1])):
        left_map = maps.reshape((-1, 2) + maps.shape[1:])[:, 0]
        left_add = adds.reshape((-1, 2) + adds.shape[1:])[:, 0]
        if excl is None:
            excl = jnp.zeros_like(left_add[:1])
            odd = left_add
        else:
            odd = jnp.einsum("tbj,tjk->tbk", excl, left_map, precision=PRECISION) + left_add
        excl = jnp.stack([excl, odd], 1).reshape((-1,) + adds.shape[1:])
    return excl


def up_sweep_adds(levels, adds):
    out = [adds]
    for maps, _ in levels[:-1]:
        pairs = maps.reshape((-1, 2) + maps.shape[1:])
        halves = adds.reshape((-1, 2) + adds.shape[1:])
        adds = (
            jnp.einsum("tbj,tjk->tbk", halves[:, 0], pairs[:, 1], precision=PRECISION)
            + halves[:, 1]
        )
        out.append(adds)
    return out


def exchanged(x, bit):
    count = lax.axis_size("tm")
    return lax.ppermute(x, "tm", [(i, i ^ bit) for i in range(count)])


def batched(lhs, rhs):
    return jnp.einsum("kij,kjl->kil", jnp.stack(lhs), jnp.stack(rhs), precision=PRECISION)


def local(observations, decay, transition, obs_map, noise_precision, smoother_gain):
    size = transition.shape[0]
    count = lax.axis_size("tm")
    index = lax.axis_index("tm")
    gain_rows = obs_map * noise_precision[:, None]
    closed_rows = transition.T - dot(transition.T, dot(obs_map.T, gain_rows))
    forward_adds = jnp.einsum("wyn,nx->wyx", observations, gain_rows, precision=PRECISION)

    following = shifted(decay[:1], -1)
    upcoming = jnp.concatenate([decay[1:], following], 0)
    step_maps = jnp.stack([decay, upcoming[::-1]])[:, :, :, None] * jnp.stack(
        [closed_rows, smoother_gain.T]
    )[:, None]

    tree = [(step_maps, forward_adds)]
    maps, adds = step_maps, forward_adds
    while maps.shape[1] > 1:
        pairs = maps.reshape((2, -1, 2) + maps.shape[2:])
        halves = adds.reshape((-1, 2) + adds.shape[1:])
        adds = (
            jnp.einsum("tbj,tjk->tbk", halves[:, 0], pairs[0, :, 1], precision=PRECISION)
            + halves[:, 1]
        )
        maps = jnp.einsum("dtij,dtjk->dtik", pairs[:, :, 0], pairs[:, :, 1], precision=PRECISION)
        tree.append((maps, adds))
    forward_tree = [(m[0], a) for m, a in tree]
    backward_tree = [(m[1], None) for m, _ in tree]

    rounds = []
    bit = 1
    while bit < count:
        rounds.append(bit)
        bit *= 2
    eye = jnp.eye(size, dtype=jnp.float32)
    total_map, total_add, before_map, before_add = maps[0, 0], adds[0], eye, jnp.zeros_like(adds[0])
    back_total, back_before = maps[1, 0], eye
    stored = []
    late = forward_tree
    for k, bit in enumerate(rounds):
        upper = (index & bit) != 0
        if k == len(rounds) - 1:
            got_add = exchanged(total_add, bit)
            entering = jnp.where(upper, dot(got_add, before_map) + before_add, before_add)
            stored.append((back_total, back_total, back_before))
            break
        message = jnp.concatenate([total_map, total_add, back_total], 0)
        got = exchanged(message, bit)
        if k == 0:
            late, got = lax.optimization_barrier((late, got))
        got_map, got_add, got_back = got[:size], got[size:-size], got[-size:]
        first_map = jnp.where(upper, got_map, total_map)
        second_map = jnp.where(upper, total_map, got_map)
        first_add = jnp.where(upper, got_add, total_add)
        second_add = jnp.where(upper, total_add, got_add)
        back_first = jnp.where(upper, back_total, got_back)
        back_second = jnp.where(upper, got_back, back_total)
        stored.append((back_total, back_second, back_before))
        products = batched(
            [first_map, got_map, back_first, got_back],
            [second_map, before_map, back_second, back_before],
        )
        offsets = batched([first_add, got_add], [second_map, before_map])
        total_map, total_add = products[0], offsets[0] + second_add
        before_map = jnp.where(upper, products[1], before_map)
        before_add = jnp.where(upper, offsets[1] + before_add, before_add)
        back_total = products[2]
        back_before = jnp.where(upper, back_before, products[3])

    excl_maps = down_sweep_maps(late)[::-1]
    excl_adds = down_sweep_adds(late, [a for _, a in late])[::-1]
    decay_back = decay[::-1][:, None, :]
    ahead_back = upcoming[::-1][:, None, :]
    previous = jnp.einsum("bs,tsr->tbr", entering, excl_maps, precision=PRECISION) + excl_adds
    filtered_back = (
        jnp.einsum("tbs,sr->tbr", previous * decay_back, closed_rows, precision=PRECISION)
        + forward_adds[::-1]
    )
    predicted = jnp.einsum(
        "tbs,sr->tbr", filtered_back * ahead_back, transition.T, precision=PRECISION
    )
    backward_adds = filtered_back - jnp.einsum(
        "tbs,sr->tbr", predicted * ahead_back, smoother_gain.T, precision=PRECISION
    )
    back_adds = up_sweep_adds(backward_tree, backward_adds)
    filtered = filtered_back[::-1]

    total_add = back_adds[-1][0]
    before_add = jnp.zeros_like(total_add)
    late_b = (backward_tree, back_adds)
    for k, bit in enumerate(rounds):
        upper = (index & bit) != 0
        own_map, second_map, own_before = stored[k]
        got_add = exchanged(total_add, bit)
        if k == 0:
            late_b, got_add = lax.optimization_barrier((late_b, got_add))
        if k == len(rounds) - 1:
            before_add = jnp.where(upper, before_add, dot(got_add, own_before) + before_add)
            break
        first_add = jnp.where(upper, total_add, got_add)
        second_add = jnp.where(upper, got_add, total_add)
        offsets = batched([first_add, got_add], [second_map, own_before])
        total_add = offsets[0] + second_add
        before_add = jnp.where(upper, before_add, offsets[1] + before_add)
    arriving = before_add
    back_excl_maps = down_sweep_maps(late_b[0])
    back_excl_adds = down_sweep_adds(late_b[0], late_b[1])
    following_state = (
        jnp.einsum("bs,tsr->tbr", arriving, back_excl_maps, precision=PRECISION) + back_excl_adds
    )
    smoothed = (
        jnp.einsum(
            "tbs,sr->tbr", following_state * ahead_back, smoother_gain.T, precision=PRECISION
        )
        + backward_adds
    )[::-1]
    return filtered, smoothed


def solution(mesh):
    in_specs = (P("tm", None, None), P("tm", None), P(), P(), P(), P())
    out_specs = (P("tm", None, None), P("tm", None, None))
    return jax.shard_map(local, mesh=mesh, in_specs=in_specs, out_specs=out_specs, check_vma=False)
```

```python
import jax
import jax.numpy as jnp
from jax import lax
from jax.sharding import PartitionSpec as P

HIGHEST = lax.Precision.HIGHEST


def dot(a, b):
    return jnp.dot(a, b, precision=HIGHEST)


def shifted(x, by):
    count = lax.axis_size("tm")
    pairs = [(i, i + by) for i in range(count) if 0 <= i + by < count]
    return lax.ppermute(x, "tm", pairs)


def step_right(x, scale, weights):
    return jnp.einsum("tbs,sr->tbr", x * scale[:, None, :], weights, precision=HIGHEST)


def pair_maps(first_scale, second_scale, weights):
    scaled = weights[None] * second_scale[:, None, :]
    product = jnp.einsum("tij,jk->tik", scaled, weights, precision=HIGHEST)
    return first_scale[:, :, None] * product


def down_sweep_maps(maps_levels, even_scale, weights):
    size = weights.shape[0]
    eye = jnp.eye(size, dtype=jnp.float32)[None]
    excl = None
    for maps in reversed(maps_levels[:-1]):
        left = maps.reshape((-1, 2) + maps.shape[1:])[:, 0]
        if excl is None:
            excl, odd = eye, left
        else:
            odd = jnp.einsum("tij,tjk->tik", excl, left, precision=HIGHEST)
        excl = interleave(excl, odd)
    if excl is None:
        excl = eye
    return interleave(excl, step_right(excl, even_scale, weights))


def down_sweep_adds(maps_levels, adds_levels, step_adds, even_scale, weights):
    excl = None
    for maps, adds in zip(reversed(maps_levels[:-1]), reversed(adds_levels[:-1])):
        left_map = maps.reshape((-1, 2) + maps.shape[1:])[:, 0]
        left_add = adds.reshape((-1, 2) + adds.shape[1:])[:, 0]
        if excl is None:
            excl, odd = jnp.zeros_like(left_add[:1]), left_add
        else:
            odd = jnp.einsum("tbj,tjk->tbk", excl, left_map, precision=HIGHEST) + left_add
        excl = interleave(excl, odd)
    if excl is None:
        excl = jnp.zeros_like(step_adds[:1])
    return interleave(excl, step_right(excl, even_scale, weights) + step_adds[0::2])


def up_sweep_adds(maps_levels, step_adds, odd_scale, weights):
    adds = step_right(step_adds[0::2], odd_scale, weights) + step_adds[1::2]
    out = [step_adds, adds]
    for maps in maps_levels[:-1]:
        pairs = maps.reshape((-1, 2) + maps.shape[1:])
        halves = adds.reshape((-1, 2) + adds.shape[1:])
        adds = (
            jnp.einsum("tbj,tjk->tbk", halves[:, 0], pairs[:, 1], precision=HIGHEST)
            + halves[:, 1]
        )
        out.append(adds)
    return out


def interleave(even, odd):
    return jnp.stack([even, odd], 1).reshape((-1,) + even.shape[1:])


def exchanged(x, bit):
    count = lax.axis_size("tm")
    return lax.ppermute(x, "tm", [(i, i ^ bit) for i in range(count)])


def batched(lhs, rhs):
    return jnp.einsum("kij,kjl->kil", jnp.stack(lhs), jnp.stack(rhs), precision=HIGHEST)


def local(observations, decay, transition, obs_map, noise_precision, smoother_gain):
    size = transition.shape[0]
    count = lax.axis_size("tm")
    index = lax.axis_index("tm")
    gain_rows = obs_map * noise_precision[:, None]
    closed_rows = transition.T - dot(transition.T, dot(obs_map.T, gain_rows))
    forward_adds = jnp.einsum("wyn,nx->wyx", observations, gain_rows, precision=HIGHEST)

    following = shifted(decay[:1], -1)
    upcoming = jnp.concatenate([decay[1:], following], 0)
    backward_scale = upcoming[::-1]
    maps = jnp.stack([
        pair_maps(decay[0::2], decay[1::2], closed_rows),
        pair_maps(backward_scale[0::2], backward_scale[1::2], smoother_gain.T),
    ])
    adds = step_right(forward_adds[0::2], decay[1::2], closed_rows) + forward_adds[1::2]
    tree = [(maps, adds)]
    while maps.shape[1] > 1:
        pairs = maps.reshape((2, -1, 2) + maps.shape[2:])
        halves = adds.reshape((-1, 2) + adds.shape[1:])
        adds = (
            jnp.einsum("tbj,tjk->tbk", halves[:, 0], pairs[0, :, 1], precision=HIGHEST)
            + halves[:, 1]
        )
        maps = jnp.einsum("dtij,dtjk->dtik", pairs[:, :, 0], pairs[:, :, 1], precision=HIGHEST)
        tree.append((maps, adds))
    forward_maps = [m[0] for m, _ in tree]
    forward_tree = (forward_maps, [a for _, a in tree])
    backward_maps = [m[1] for m, _ in tree]

    rounds = []
    bit = 1
    while bit < count:
        rounds.append(bit)
        bit *= 2
    eye = jnp.eye(size, dtype=jnp.float32)
    total_map, total_add, before_map, before_add = maps[0, 0], adds[0], eye, jnp.zeros_like(adds[0])
    back_total, back_before = maps[1, 0], eye
    stored = []
    late = forward_tree
    for k, bit in enumerate(rounds):
        upper = (index & bit) != 0
        if k == len(rounds) - 1:
            got_add = exchanged(total_add, bit)
            entering = jnp.where(upper, dot(got_add, before_map) + before_add, before_add)
            stored.append((back_total, back_total, back_before))
            break
        message = jnp.concatenate([total_map, total_add, back_total], 0)
        got = exchanged(message, bit)
        if k == 0:
            late, got = lax.optimization_barrier((late, got))
        got_map, got_add, got_back = got[:size], got[size:-size], got[-size:]
        first_map = jnp.where(upper, got_map, total_map)
        second_map = jnp.where(upper, total_map, got_map)
        first_add = jnp.where(upper, got_add, total_add)
        second_add = jnp.where(upper, total_add, got_add)
        back_first = jnp.where(upper, back_total, got_back)
        back_second = jnp.where(upper, got_back, back_total)
        stored.append((back_total, back_second, back_before))
        products = batched(
            [first_map, got_map, back_first, got_back],
            [second_map, before_map, back_second, back_before],
        )
        offsets = batched([first_add, got_add], [second_map, before_map])
        total_map, total_add = products[0], offsets[0] + second_add
        before_map = jnp.where(upper, products[1], before_map)
        before_add = jnp.where(upper, offsets[1] + before_add, before_add)
        back_total = products[2]
        back_before = jnp.where(upper, back_before, products[3])

    excl_maps = down_sweep_maps(late[0], decay[0::2], closed_rows)
    excl_adds = down_sweep_adds(late[0], late[1], forward_adds, decay[0::2], closed_rows)
    previous = jnp.einsum("bs,tsr->tbr", entering, excl_maps, precision=HIGHEST) + excl_adds
    filtered = (
        jnp.einsum("tbs,sr->tbr", previous * decay[:, None, :], closed_rows, precision=HIGHEST)
        + forward_adds
    )
    predicted = jnp.einsum(
        "tbs,sr->tbr", filtered * upcoming[:, None, :], transition.T, precision=HIGHEST
    )
    backward_adds = filtered - jnp.einsum(
        "tbs,sr->tbr", predicted * upcoming[:, None, :], smoother_gain.T, precision=HIGHEST
    )
    back_adds = up_sweep_adds(backward_maps, backward_adds[::-1], backward_scale[1::2], smoother_gain.T)

    total_add = back_adds[-1][0]
    before_add = jnp.zeros_like(total_add)
    late_b = (backward_maps, back_adds)
    for k, bit in enumerate(rounds):
        upper = (index & bit) != 0
        own_map, second_map, own_before = stored[k]
        got_add = exchanged(total_add, bit)
        if k == 0:
            late_b, got_add = lax.optimization_barrier((late_b, got_add))
        if k == len(rounds) - 1:
            before_add = jnp.where(upper, before_add, dot(got_add, own_before) + before_add)
            break
        first_add = jnp.where(upper, total_add, got_add)
        second_add = jnp.where(upper, got_add, total_add)
        offsets = batched([first_add, got_add], [second_map, own_before])
        total_add = offsets[0] + second_add
        before_add = jnp.where(upper, before_add, offsets[1] + before_add)
    arriving = before_add
    back_excl_maps = down_sweep_maps(late_b[0], backward_scale[0::2], smoother_gain.T)
    back_excl_adds = down_sweep_adds(
        late_b[0], late_b[1][1:], late_b[1][0], backward_scale[0::2], smoother_gain.T
    )
    following_state = (
        jnp.einsum("bs,tsr->tbr", arriving, back_excl_maps, precision=HIGHEST) + back_excl_adds
    )[::-1]
    smoothed = (
        jnp.einsum(
            "tbs,sr->tbr", following_state * upcoming[:, None, :], smoother_gain.T, precision=HIGHEST
        )
        + backward_adds
    )
    return filtered, smoothed


def solution(mesh):
    in_specs = (P("tm", None, None), P("tm", None), P(), P(), P(), P())
    out_specs = (P("tm", None, None), P("tm", None, None))
    return jax.shard_map(local, mesh=mesh, in_specs=in_specs, out_specs=out_specs, check_vma=False)
```

```python
import jax
import jax.numpy as jnp
from jax import lax
from jax.sharding import PartitionSpec as P

HIGHEST = lax.Precision.HIGHEST


def dot(a, b):
    return jnp.dot(a, b, precision=HIGHEST)


def shifted(x, by):
    count = lax.axis_size("tm")
    pairs = [(i, i + by) for i in range(count) if 0 <= i + by < count]
    return lax.ppermute(x, "tm", pairs)


def step_right(x, scale, weights):
    return jnp.einsum("tbs,sr->tbr", x * scale[:, None, :], weights, precision=HIGHEST)


def pair_maps(first_scale, second_scale, weights):
    scaled = weights[None] * second_scale[:, None, :]
    product = jnp.einsum("tij,jk->tik", scaled, weights, precision=HIGHEST)
    return first_scale[:, :, None] * product


def down_sweep_maps(maps_levels, even_scale, weights):
    size = weights.shape[0]
    eye = jnp.eye(size, dtype=jnp.float32)[None]
    excl = None
    for maps in reversed(maps_levels[:-1]):
        left = maps.reshape((-1, 2) + maps.shape[1:])[:, 0]
        if excl is None:
            excl, odd = eye, left
        else:
            odd = jnp.einsum("tij,tjk->tik", excl, left, precision=HIGHEST)
        excl = interleave(excl, odd)
    if excl is None:
        excl = eye
    return interleave(excl, step_right(excl, even_scale, weights))


def down_sweep_adds(maps_levels, adds_levels, step_adds, even_scale, weights):
    excl = None
    for maps, adds in zip(reversed(maps_levels[:-1]), reversed(adds_levels[:-1])):
        left_map = maps.reshape((-1, 2) + maps.shape[1:])[:, 0]
        left_add = adds.reshape((-1, 2) + adds.shape[1:])[:, 0]
        if excl is None:
            excl, odd = jnp.zeros_like(left_add[:1]), left_add
        else:
            odd = jnp.einsum("tbj,tjk->tbk", excl, left_map, precision=HIGHEST) + left_add
        excl = interleave(excl, odd)
    if excl is None:
        excl = jnp.zeros_like(step_adds[:1])
    return interleave(excl, step_right(excl, even_scale, weights) + step_adds[0::2])


def up_sweep_adds(maps_levels, step_adds, odd_scale, weights):
    adds = step_right(step_adds[0::2], odd_scale, weights) + step_adds[1::2]
    out = [step_adds, adds]
    for maps in maps_levels[:-1]:
        pairs = maps.reshape((-1, 2) + maps.shape[1:])
        halves = adds.reshape((-1, 2) + adds.shape[1:])
        adds = (
            jnp.einsum("tbj,tjk->tbk", halves[:, 0], pairs[:, 1], precision=HIGHEST)
            + halves[:, 1]
        )
        out.append(adds)
    return out


def interleave(even, odd):
    return jnp.stack([even, odd], 1).reshape((-1,) + even.shape[1:])


def partner(i, bit):
    if bit >= 4 and (bit.bit_length() - 1) % 2 == 0:
        low = bit // 2
        position = (i // low) % 4
        return i + (3 - 2 * position) * low
    return i ^ bit


def exchanged(x, bit):
    count = lax.axis_size("tm")
    return lax.ppermute(x, "tm", [(i, partner(i, bit)) for i in range(count)])


def batched(lhs, rhs):
    return jnp.einsum("kij,kjl->kil", jnp.stack(lhs), jnp.stack(rhs), precision=HIGHEST)


def local(observations, decay, transition, obs_map, noise_precision, smoother_gain):
    size = transition.shape[0]
    count = lax.axis_size("tm")
    index = lax.axis_index("tm")
    gain_rows = obs_map * noise_precision[:, None]
    closed_rows = transition.T - dot(transition.T, dot(obs_map.T, gain_rows))
    forward_adds = jnp.einsum("wyn,nx->wyx", observations, gain_rows, precision=HIGHEST)

    following = shifted(decay[:1], -1)
    upcoming = jnp.concatenate([decay[1:], following], 0)
    backward_scale = upcoming[::-1]
    maps = jnp.stack([
        pair_maps(decay[0::2], decay[1::2], closed_rows),
        pair_maps(backward_scale[0::2], backward_scale[1::2], smoother_gain.T),
    ])
    adds = step_right(forward_adds[0::2], decay[1::2], closed_rows) + forward_adds[1::2]
    tree = [(maps, adds)]
    while maps.shape[1] > 1:
        pairs = maps.reshape((2, -1, 2) + maps.shape[2:])
        halves = adds.reshape((-1, 2) + adds.shape[1:])
        adds = (
            jnp.einsum("tbj,tjk->tbk", halves[:, 0], pairs[0, :, 1], precision=HIGHEST)
            + halves[:, 1]
        )
        maps = jnp.einsum("dtij,dtjk->dtik", pairs[:, :, 0], pairs[:, :, 1], precision=HIGHEST)
        tree.append((maps, adds))
    forward_maps = [m[0] for m, _ in tree]
    forward_tree = (forward_maps, [a for _, a in tree])
    backward_maps = [m[1] for m, _ in tree]

    rounds = []
    bit = 1
    while bit < count:
        rounds.append(bit)
        bit *= 2
    eye = jnp.eye(size, dtype=jnp.float32)
    total_map, total_add, before_map, before_add = maps[0, 0], adds[0], eye, jnp.zeros_like(adds[0])
    back_total, back_before = maps[1, 0], eye
    stored = []
    late = forward_tree
    for k, bit in enumerate(rounds):
        upper = (index & bit) != 0
        if k == len(rounds) - 1:
            got_add = exchanged(total_add, bit)
            entering = jnp.where(upper, dot(got_add, before_map) + before_add, before_add)
            stored.append((back_total, back_total, back_before))
            break
        message = jnp.concatenate([total_map, total_add, back_total], 0)
        got = exchanged(message, bit)
        if k == 0:
            late, got = lax.optimization_barrier((late, got))
        got_map, got_add, got_back = got[:size], got[size:-size], got[-size:]
        first_map = jnp.where(upper, got_map, total_map)
        second_map = jnp.where(upper, total_map, got_map)
        first_add = jnp.where(upper, got_add, total_add)
        second_add = jnp.where(upper, total_add, got_add)
        back_first = jnp.where(upper, back_total, got_back)
        back_second = jnp.where(upper, got_back, back_total)
        stored.append((back_total, back_second, back_before))
        products = batched(
            [first_map, got_map, back_first, got_back],
            [second_map, before_map, back_second, back_before],
        )
        offsets = batched([first_add, got_add], [second_map, before_map])
        total_map, total_add = products[0], offsets[0] + second_add
        before_map = jnp.where(upper, products[1], before_map)
        before_add = jnp.where(upper, offsets[1] + before_add, before_add)
        back_total = products[2]
        back_before = jnp.where(upper, back_before, products[3])

    excl_maps = down_sweep_maps(late[0], decay[0::2], closed_rows)
    excl_adds = down_sweep_adds(late[0], late[1], forward_adds, decay[0::2], closed_rows)
    previous = jnp.einsum("bs,tsr->tbr", entering, excl_maps, precision=HIGHEST) + excl_adds
    filtered = (
        jnp.einsum("tbs,sr->tbr", previous * decay[:, None, :], closed_rows, precision=HIGHEST)
        + forward_adds
    )
    predicted = jnp.einsum(
        "tbs,sr->tbr", filtered * upcoming[:, None, :], transition.T, precision=HIGHEST
    )
    backward_adds = filtered - jnp.einsum(
        "tbs,sr->tbr", predicted * upcoming[:, None, :], smoother_gain.T, precision=HIGHEST
    )
    back_adds = up_sweep_adds(backward_maps, backward_adds[::-1], backward_scale[1::2], smoother_gain.T)

    total_add = back_adds[-1][0]
    before_add = jnp.zeros_like(total_add)
    late_b = (backward_maps, back_adds)
    for k, bit in enumerate(rounds):
        upper = (index & bit) != 0
        own_map, second_map, own_before = stored[k]
        got_add = exchanged(total_add, bit)
        if k == 0:
            late_b, got_add = lax.optimization_barrier((late_b, got_add))
        if k == len(rounds) - 1:
            before_add = jnp.where(upper, before_add, dot(got_add, own_before) + before_add)
            break
        first_add = jnp.where(upper, total_add, got_add)
        second_add = jnp.where(upper, got_add, total_add)
        offsets = batched([first_add, got_add], [second_map, own_before])
        total_add = offsets[0] + second_add
        before_add = jnp.where(upper, before_add, offsets[1] + before_add)
    arriving = before_add
    back_excl_maps = down_sweep_maps(late_b[0], backward_scale[0::2], smoother_gain.T)
    back_excl_adds = down_sweep_adds(
        late_b[0], late_b[1][1:], late_b[1][0], backward_scale[0::2], smoother_gain.T
    )
    following_state = (
        jnp.einsum("bs,tsr->tbr", arriving, back_excl_maps, precision=HIGHEST) + back_excl_adds
    )[::-1]
    smoothed = (
        jnp.einsum(
            "tbs,sr->tbr", following_state * upcoming[:, None, :], smoother_gain.T, precision=HIGHEST
        )
        + backward_adds
    )
    return filtered, smoothed


def solution(mesh):
    in_specs = (P("tm", None, None), P("tm", None), P(), P(), P(), P())
    out_specs = (P("tm", None, None), P("tm", None, None))
    return jax.shard_map(local, mesh=mesh, in_specs=in_specs, out_specs=out_specs, check_vma=False)
```

```python
import jax
import jax.numpy as jnp
from jax import lax
from jax.sharding import PartitionSpec as P

HIGHEST = lax.Precision.HIGHEST


def dot(a, b):
    return jnp.dot(a, b, precision=HIGHEST)


def bmm(a, b):
    return jnp.einsum("...ij,...jk->...ik", a, b, precision=HIGHEST)


def shifted(x, by):
    count = lax.axis_size("tm")
    pairs = [(i, i + by) for i in range(count) if 0 <= i + by < count]
    return lax.ppermute(x, "tm", pairs)


def step_right(x, scale, weights):
    return jnp.einsum("tbs,sr->tbr", x * scale[:, None, :], weights, precision=HIGHEST)


def pair_maps(first_scale, second_scale, weights):
    scaled = weights[None] * second_scale[:, None, :]
    product = jnp.einsum("tij,jk->tik", scaled, weights, precision=HIGHEST)
    return first_scale[:, :, None] * product


def down_sweep_maps(maps_levels, even_scale, weights):
    size = weights.shape[0]
    eye = jnp.eye(size, dtype=jnp.float32)[None]
    excl = None
    for maps in reversed(maps_levels[:-1]):
        left = maps.reshape((-1, 2) + maps.shape[1:])[:, 0]
        if excl is None:
            excl, odd = eye, left
        else:
            odd = jnp.einsum("tij,tjk->tik", excl, left, precision=HIGHEST)
        excl = interleave(excl, odd)
    if excl is None:
        excl = eye
    return interleave(excl, step_right(excl, even_scale, weights))


def down_sweep_adds(maps_levels, adds_levels, step_adds, even_scale, weights):
    excl = None
    for maps, adds in zip(reversed(maps_levels[:-1]), reversed(adds_levels[:-1])):
        left_map = maps.reshape((-1, 2) + maps.shape[1:])[:, 0]
        left_add = adds.reshape((-1, 2) + adds.shape[1:])[:, 0]
        if excl is None:
            excl, odd = jnp.zeros_like(left_add[:1]), left_add
        else:
            odd = jnp.einsum("tbj,tjk->tbk", excl, left_map, precision=HIGHEST) + left_add
        excl = interleave(excl, odd)
    if excl is None:
        excl = jnp.zeros_like(step_adds[:1])
    return interleave(excl, step_right(excl, even_scale, weights) + step_adds[0::2])


def up_sweep_adds(maps_levels, step_adds, odd_scale, weights):
    adds = step_right(step_adds[0::2], odd_scale, weights) + step_adds[1::2]
    out = [step_adds, adds]
    for maps in maps_levels[:-1]:
        pairs = maps.reshape((-1, 2) + maps.shape[1:])
        halves = adds.reshape((-1, 2) + adds.shape[1:])
        adds = (
            jnp.einsum("tbj,tjk->tbk", halves[:, 0], pairs[:, 1], precision=HIGHEST)
            + halves[:, 1]
        )
        out.append(adds)
    return out


def interleave(even, odd):
    return jnp.stack([even, odd], 1).reshape((-1,) + even.shape[1:])


def partner(i, bit):
    if bit >= 4 and (bit.bit_length() - 1) % 2 == 0:
        low = bit // 2
        position = (i // low) % 4
        return i + (3 - 2 * position) * low
    return i ^ bit


def exchanged(x, bit):
    count = lax.axis_size("tm")
    return lax.ppermute(x, "tm", [(i, partner(i, bit)) for i in range(count)])


def batched(lhs, rhs):
    return jnp.einsum("kij,kjl->kil", jnp.stack(lhs), jnp.stack(rhs), precision=HIGHEST)


def pair_pairs(x):
    return x.reshape((-1, 2) + x.shape[1:])


def merge_levels(node):
    F, f, B, K, k = (pair_pairs(x) for x in node)
    F1, f1, B1, K1, k1 = F[:, 0], f[:, 0], B[:, 0], K[:, 0], k[:, 0]
    F2, f2, B2, K2, k2 = F[:, 1], f[:, 1], B[:, 1], K[:, 1], k[:, 1]
    lead = jnp.einsum(
        "dtij,dtjk->dtik", jnp.stack([F1, F1, B2]), jnp.stack([F2, K2, B1]), precision=HIGHEST
    )
    lead_add = jnp.einsum("tbj,dtjk->dtbk", f1, jnp.stack([F2, K2]), precision=HIGHEST)
    cross = jnp.einsum("tij,tjk->tik", lead[1], B1, precision=HIGHEST)
    cross_add = jnp.einsum("tbj,tjk->tbk", lead_add[1] + k2, B1, precision=HIGHEST)
    return (lead[0], lead_add[0] + f2, lead[2], cross + K1, cross_add + k1)


def local(observations, decay, transition, obs_map, noise_precision, smoother_gain):
    size = transition.shape[0]
    count = lax.axis_size("tm")
    index = lax.axis_index("tm")
    gain_rows = obs_map * noise_precision[:, None]
    closed_rows = transition.T - dot(transition.T, dot(obs_map.T, gain_rows))
    forward_adds = jnp.einsum("wyn,nx->wyx", observations, gain_rows, precision=HIGHEST)
    transition_t = transition.T
    gain_t = smoother_gain.T

    following = shifted(decay[:1], -1)
    upcoming = jnp.concatenate([decay[1:], following], 0)
    ahead = upcoming[:, None, :]

    def shared(x, weights):
        return jnp.einsum("tij,jk->tik", x, weights, precision=HIGHEST)

    def residual(v):
        return v - shared(shared(v * ahead, transition_t) * ahead, gain_t)

    step_cross = residual(decay[:, :, None] * closed_rows[None])
    step_cross_add = residual(forward_adds)
    d_e, d_o = decay[0::2], decay[1::2]
    a_e, a_o = upcoming[0::2], upcoming[1::2]
    b_e, b_o = forward_adds[0::2], forward_adds[1::2]
    K_e, K_o = step_cross[0::2], step_cross[1::2]
    k_e, k_o = step_cross_add[0::2], step_cross_add[1::2]
    cross_lead = d_e[:, :, None] * jnp.einsum("ij,tjk->tik", closed_rows, K_o, precision=HIGHEST)
    cross_lead_add = jnp.einsum("tbj,tjk->tbk", b_e, K_o, precision=HIGHEST) + k_o
    node = (
        pair_maps(d_e, d_o, closed_rows),
        step_right(b_e, d_o, closed_rows) + b_o,
        pair_maps(a_o, a_e, gain_t),
        shared(cross_lead * a_e[:, None, :], gain_t) + K_e,
        step_right(cross_lead_add, a_e, gain_t) + k_e,
    )
    levels = [node]
    while node[0].shape[0] > 1:
        node = merge_levels(node)
        levels.append(node)
    total = tuple(x[0] for x in node)
    rows = total[1].shape[0]

    eye = jnp.eye(size, dtype=jnp.float32)
    zero_add = jnp.zeros_like(total[1])
    before_map, before_add = eye, zero_add
    after_map, after_cross, after_add = eye, jnp.zeros_like(eye), zero_add
    rounds = []
    bit = 1
    while bit < count:
        rounds.append(bit)
        bit *= 2
    late = levels
    for k, bit in enumerate(rounds):
        upper = (index & bit) != 0
        if k == len(rounds) - 1:
            got = exchanged(jnp.concatenate([total[3], total[1], total[4]], 0), bit)
            got_cross, got_add, got_cross_add = got[:size], got[size:size + rows], got[size + rows:]
            lower_add = jnp.where(upper, got_add, total[1])
            upper_cross = jnp.where(upper, total[3], got_cross)
            upper_cross_add = jnp.where(upper, total[4], got_cross_add)
            products = bmm(lower_add, jnp.stack([before_map, after_cross, upper_cross]))
            entering = jnp.where(upper, products[0] + before_add, before_add)
            arriving = jnp.where(
                upper,
                products[1] + after_add,
                dot(products[2] + upper_cross_add, after_map) + after_add,
            )
            break
        F, f, B, K, kk = total
        got = exchanged(jnp.concatenate([F, B, K, f, kk], 0), bit)
        if k == 0:
            late, got = lax.optimization_barrier((late, got))
        got = (
            got[:size],
            got[3 * size:3 * size + rows],
            got[size:2 * size],
            got[2 * size:3 * size],
            got[3 * size + rows:],
        )
        lower = tuple(jnp.where(upper, g, t) for g, t in zip(got, total))
        higher = tuple(jnp.where(upper, t, g) for g, t in zip(got, total))
        LF, Lf, LB, LK, Lk = lower
        UF, Uf, UB, UK, Uk = higher
        lead = bmm(
            jnp.stack([LF, LF, UB, LF, LF, UB]),
            jnp.stack([UF, UK, LB, before_map, after_cross, after_map]),
        )
        lead_add = bmm(Lf, jnp.stack([UF, UK, before_map, after_cross]))
        cross_add = lead_add[1] + Uk
        tail = bmm(jnp.stack([lead[1], lead[1]]), jnp.stack([LB, after_map]))
        tail_add = bmm(cross_add, jnp.stack([LB, after_map]))
        total = (lead[0], lead_add[0] + Uf, lead[2], tail[0] + LK, tail_add[0] + Lk)
        before_map = jnp.where(upper, lead[3], before_map)
        before_add = jnp.where(upper, lead_add[2] + before_add, before_add)
        after_cross = jnp.where(upper, lead[4], tail[1] + after_cross)
        after_add = jnp.where(upper, lead_add[3] + after_add, tail_add[1] + after_add)
        after_map = jnp.where(upper, after_map, lead[5])

    maps_levels = [n[0] for n in late]
    prefix_maps = down_sweep_maps(maps_levels, d_e, closed_rows)
    prefix_adds = down_sweep_adds(maps_levels, [n[1] for n in late], forward_adds, d_e, closed_rows)

    after = None
    for node in reversed(late[:-1]):
        F, f, B, K, kk = (pair_pairs(x)[:, 1] for x in node)
        if after is None:
            left_after = (B, K, kk)
            right_after = (eye[None], jnp.zeros_like(eye)[None], jnp.zeros_like(kk[:1]))
        else:
            B2, K2, k2 = after
            lead = bmm(jnp.stack([F, B2]), jnp.stack([K2, B]))
            lead_add = bmm(f, K2) + k2
            left_after = (lead[1], bmm(lead[0], B) + K, bmm(lead_add, B) + kk)
            right_after = after
        after = tuple(interleave(l, r) for l, r in zip(left_after, right_after))
    B2, K2, k2 = after
    scaled_cross = d_o[:, :, None] * jnp.einsum("ij,tjk->tik", closed_rows, K2, precision=HIGHEST)
    left_after = (
        shared(B2 * a_o[:, None, :], gain_t),
        shared(scaled_cross * a_o[:, None, :], gain_t) + K_o,
        step_right(bmm(b_o, K2) + k2, a_o, gain_t) + k_o,
    )
    suffix_maps, suffix_cross, suffix_adds = (
        interleave(l, r) for l, r in zip(left_after, after)
    )

    previous = jnp.einsum("bs,tsr->tbr", entering, prefix_maps, precision=HIGHEST) + prefix_adds
    filtered = (
        jnp.einsum("tbs,sr->tbr", previous * decay[:, None, :], closed_rows, precision=HIGHEST)
        + forward_adds
    )
    following_state = (
        jnp.einsum("bs,tsr->tbr", arriving, suffix_maps, precision=HIGHEST)
        + bmm(filtered, suffix_cross)
        + suffix_adds
    )
    predicted = jnp.einsum("tbs,sr->tbr", filtered * ahead, transition_t, precision=HIGHEST)
    smoothed = filtered + jnp.einsum(
        "tbs,sr->tbr", (following_state - predicted) * ahead, gain_t, precision=HIGHEST
    )
    return filtered, smoothed


def solution(mesh):
    in_specs = (P("tm", None, None), P("tm", None), P(), P(), P(), P())
    out_specs = (P("tm", None, None), P("tm", None, None))
    return jax.shard_map(local, mesh=mesh, in_specs=in_specs, out_specs=out_specs, check_vma=False)
```

```python
import jax
import jax.numpy as jnp
from jax import lax
from jax.sharding import PartitionSpec as P

HIGHEST = lax.Precision.HIGHEST


def dot(a, b):
    return jnp.dot(a, b, precision=HIGHEST)


def shifted(x, by):
    count = lax.axis_size("tm")
    pairs = [(i, i + by) for i in range(count) if 0 <= i + by < count]
    return lax.ppermute(x, "tm", pairs)


def step_right(x, scale, weights):
    return jnp.einsum("tbs,sr->tbr", x * scale[:, None, :], weights, precision=HIGHEST)


def pair_maps(first_scale, second_scale, weights):
    scaled = weights[None] * second_scale[:, None, :]
    product = jnp.einsum("tij,jk->tik", scaled, weights, precision=HIGHEST)
    return first_scale[:, :, None] * product


def down_sweep_maps(maps_levels, even_scale, weights):
    size = weights.shape[0]
    eye = jnp.eye(size, dtype=jnp.float32)[None]
    excl = None
    for maps in reversed(maps_levels[:-1]):
        left = maps.reshape((-1, 2) + maps.shape[1:])[:, 0]
        if excl is None:
            excl, odd = eye, left
        else:
            odd = jnp.einsum("tij,tjk->tik", excl, left, precision=HIGHEST)
        excl = interleave(excl, odd)
    if excl is None:
        excl = eye
    return interleave(excl, step_right(excl, even_scale, weights))


def down_sweep_adds(maps_levels, adds_levels, step_adds, even_scale, weights):
    excl = None
    for maps, adds in zip(reversed(maps_levels[:-1]), reversed(adds_levels[:-1])):
        left_map = maps.reshape((-1, 2) + maps.shape[1:])[:, 0]
        left_add = adds.reshape((-1, 2) + adds.shape[1:])[:, 0]
        if excl is None:
            excl, odd = jnp.zeros_like(left_add[:1]), left_add
        else:
            odd = jnp.einsum("tbj,tjk->tbk", excl, left_map, precision=HIGHEST) + left_add
        excl = interleave(excl, odd)
    if excl is None:
        excl = jnp.zeros_like(step_adds[:1])
    return interleave(excl, step_right(excl, even_scale, weights) + step_adds[0::2])


def up_sweep_adds(maps_levels, step_adds, odd_scale, weights):
    adds = step_right(step_adds[0::2], odd_scale, weights) + step_adds[1::2]
    out = [step_adds, adds]
    for maps in maps_levels[:-1]:
        pairs = maps.reshape((-1, 2) + maps.shape[1:])
        halves = adds.reshape((-1, 2) + adds.shape[1:])
        adds = (
            jnp.einsum("tbj,tjk->tbk", halves[:, 0], pairs[:, 1], precision=HIGHEST)
            + halves[:, 1]
        )
        out.append(adds)
    return out


def interleave(even, odd):
    return jnp.stack([even, odd], 1).reshape((-1,) + even.shape[1:])


def partner(i, bit):
    if bit >= 4 and (bit.bit_length() - 1) % 2 == 0:
        low = bit // 2
        position = (i // low) % 4
        return i + (3 - 2 * position) * low
    return i ^ bit


def exchanged(x, bit):
    count = lax.axis_size("tm")
    return lax.ppermute(x, "tm", [(i, partner(i, bit)) for i in range(count)])


def batched(lhs, rhs):
    return jnp.einsum("kij,kjl->kil", jnp.stack(lhs), jnp.stack(rhs), precision=HIGHEST)


def local(observations, decay, transition, obs_map, noise_precision, smoother_gain):
    size = transition.shape[0]
    count = lax.axis_size("tm")
    index = lax.axis_index("tm")
    gain_rows = obs_map * noise_precision[:, None]
    closed_rows = transition.T - dot(transition.T, dot(obs_map.T, gain_rows))
    forward_adds = jnp.einsum("wyn,nx->wyx", observations, gain_rows, precision=HIGHEST)

    following = shifted(decay[:1], -1)
    upcoming = jnp.concatenate([decay[1:], following], 0)
    backward_scale = upcoming[::-1]
    decay_pairs = decay.reshape((-1, 2) + decay.shape[1:])
    scale_pairs = backward_scale.reshape((-1, 2) + backward_scale.shape[1:])
    adds_pairs = forward_adds.reshape((-1, 2) + forward_adds.shape[1:])
    maps = jnp.stack([
        pair_maps(decay_pairs[:, 0], decay_pairs[:, 1], closed_rows),
        pair_maps(scale_pairs[:, 0], scale_pairs[:, 1], smoother_gain.T),
    ])
    adds = step_right(adds_pairs[:, 0], decay_pairs[:, 1], closed_rows) + adds_pairs[:, 1]
    tree = [(maps, adds)]
    while maps.shape[1] > 1:
        pairs = maps.reshape((2, -1, 2) + maps.shape[2:])
        halves = adds.reshape((-1, 2) + adds.shape[1:])
        adds = (
            jnp.einsum("tbj,tjk->tbk", halves[:, 0], pairs[0, :, 1], precision=HIGHEST)
            + halves[:, 1]
        )
        maps = jnp.einsum("dtij,dtjk->dtik", pairs[:, :, 0], pairs[:, :, 1], precision=HIGHEST)
        tree.append((maps, adds))
    forward_maps = [m[0] for m, _ in tree]
    forward_tree = (forward_maps, [a for _, a in tree])
    backward_maps = [m[1] for m, _ in tree]

    rounds = []
    bit = 1
    while bit < count:
        rounds.append(bit)
        bit *= 2
    eye = jnp.eye(size, dtype=jnp.float32)
    total_map, total_add, before_map, before_add = maps[0, 0], adds[0], eye, jnp.zeros_like(adds[0])
    back_total, back_before = maps[1, 0], eye
    stored = []
    late = forward_tree
    for k, bit in enumerate(rounds):
        upper = (index & bit) != 0
        if k == len(rounds) - 1:
            got_add = exchanged(total_add, bit)
            entering = jnp.where(upper, dot(got_add, before_map) + before_add, before_add)
            stored.append((back_total, back_total, back_before))
            break
        message = jnp.concatenate([total_map, total_add, back_total], 0)
        got = exchanged(message, bit)
        if k == 0:
            late, got = lax.optimization_barrier((late, got))
        got_map, got_add, got_back = got[:size], got[size:-size], got[-size:]
        first_map = jnp.where(upper, got_map, total_map)
        second_map = jnp.where(upper, total_map, got_map)
        first_add = jnp.where(upper, got_add, total_add)
        second_add = jnp.where(upper, total_add, got_add)
        back_first = jnp.where(upper, back_total, got_back)
        back_second = jnp.where(upper, got_back, back_total)
        stored.append((back_total, back_second, back_before))
        products = batched(
            [first_map, got_map, back_first, got_back],
            [second_map, before_map, back_second, back_before],
        )
        offsets = batched([first_add, got_add], [second_map, before_map])
        total_map, total_add = products[0], offsets[0] + second_add
        before_map = jnp.where(upper, products[1], before_map)
        before_add = jnp.where(upper, offsets[1] + before_add, before_add)
        back_total = products[2]
        back_before = jnp.where(upper, back_before, products[3])

    excl_maps = down_sweep_maps(late[0], decay[0::2], closed_rows)
    excl_adds = down_sweep_adds(late[0], late[1], forward_adds, decay[0::2], closed_rows)
    previous = jnp.einsum("bs,tsr->tbr", entering, excl_maps, precision=HIGHEST) + excl_adds
    filtered = (
        jnp.einsum("tbs,sr->tbr", previous * decay[:, None, :], closed_rows, precision=HIGHEST)
        + forward_adds
    )
    predicted = jnp.einsum(
        "tbs,sr->tbr", filtered * upcoming[:, None, :], transition.T, precision=HIGHEST
    )
    backward_adds = filtered - jnp.einsum(
        "tbs,sr->tbr", predicted * upcoming[:, None, :], smoother_gain.T, precision=HIGHEST
    )
    back_adds = up_sweep_adds(backward_maps, backward_adds[::-1], backward_scale[1::2], smoother_gain.T)

    total_add = back_adds[-1][0]
    before_add = jnp.zeros_like(total_add)
    late_b = (backward_maps, back_adds)
    for k, bit in enumerate(rounds):
        upper = (index & bit) != 0
        own_map, second_map, own_before = stored[k]
        got_add = exchanged(total_add, bit)
        if k == 0:
            late_b, got_add = lax.optimization_barrier((late_b, got_add))
        if k == len(rounds) - 1:
            before_add = jnp.where(upper, before_add, dot(got_add, own_before) + before_add)
            break
        first_add = jnp.where(upper, total_add, got_add)
        second_add = jnp.where(upper, got_add, total_add)
        offsets = batched([first_add, got_add], [second_map, own_before])
        total_add = offsets[0] + second_add
        before_add = jnp.where(upper, before_add, offsets[1] + before_add)
    arriving = before_add
    back_excl_maps = down_sweep_maps(late_b[0], backward_scale[0::2], smoother_gain.T)
    back_excl_adds = down_sweep_adds(
        late_b[0], late_b[1][1:], late_b[1][0], backward_scale[0::2], smoother_gain.T
    )
    following_state = (
        jnp.einsum("bs,tsr->tbr", arriving, back_excl_maps, precision=HIGHEST) + back_excl_adds
    )[::-1]
    smoothed = (
        jnp.einsum(
            "tbs,sr->tbr", following_state * upcoming[:, None, :], smoother_gain.T, precision=HIGHEST
        )
        + backward_adds
    )
    return filtered, smoothed


def solution(mesh):
    in_specs = (P("tm", None, None), P("tm", None), P(), P(), P(), P())
    out_specs = (P("tm", None, None), P("tm", None, None))
    return jax.shard_map(local, mesh=mesh, in_specs=in_specs, out_specs=out_specs, check_vma=False)
```

```python
import jax
import jax.numpy as jnp
from jax import lax
from jax.sharding import PartitionSpec as P

HIGHEST = lax.Precision.HIGHEST


def dot(a, b):
    return jnp.dot(a, b, precision=HIGHEST)


def shifted(x, by):
    count = lax.axis_size("tm")
    pairs = [(i, i + by) for i in range(count) if 0 <= i + by < count]
    return lax.ppermute(x, "tm", pairs)


def step_right(x, scale, weights):
    return jnp.einsum("tbs,sr->tbr", x * scale[:, None, :], weights, precision=HIGHEST)


def pair_maps(first_scale, second_scale, weights):
    scaled = weights[None] * second_scale[:, None, :]
    product = jnp.einsum("tij,jk->tik", scaled, weights, precision=HIGHEST)
    return first_scale[:, :, None] * product


def down_sweep_maps(maps_levels, even_scale, weights):
    size = weights.shape[0]
    eye = jnp.eye(size, dtype=jnp.float32)[None]
    excl = None
    for maps in reversed(maps_levels[:-1]):
        left = maps.reshape((-1, 2) + maps.shape[1:])[:, 0]
        if excl is None:
            excl, odd = eye, left
        else:
            odd = jnp.einsum("tij,tjk->tik", excl, left, precision=HIGHEST)
        excl = interleave(excl, odd)
    if excl is None:
        excl = eye
    return interleave(excl, step_right(excl, even_scale, weights))


def down_sweep_adds(maps_levels, adds_levels, step_adds, even_scale, weights):
    excl = None
    for maps, adds in zip(reversed(maps_levels[:-1]), reversed(adds_levels[:-1])):
        left_map = maps.reshape((-1, 2) + maps.shape[1:])[:, 0]
        left_add = adds.reshape((-1, 2) + adds.shape[1:])[:, 0]
        if excl is None:
            excl, odd = jnp.zeros_like(left_add[:1]), left_add
        else:
            odd = jnp.einsum("tbj,tjk->tbk", excl, left_map, precision=HIGHEST) + left_add
        excl = interleave(excl, odd)
    if excl is None:
        excl = jnp.zeros_like(step_adds[:1])
    return interleave(excl, step_right(excl, even_scale, weights) + step_adds[0::2])


def up_sweep_adds(maps_levels, step_adds, odd_scale, weights):
    adds = step_right(step_adds[0::2], odd_scale, weights) + step_adds[1::2]
    out = [step_adds, adds]
    for maps in maps_levels[:-1]:
        pairs = maps.reshape((-1, 2) + maps.shape[1:])
        halves = adds.reshape((-1, 2) + adds.shape[1:])
        adds = (
            jnp.einsum("tbj,tjk->tbk", halves[:, 0], pairs[:, 1], precision=HIGHEST)
            + halves[:, 1]
        )
        out.append(adds)
    return out


def down_level(state, maps, adds):
    left_map = maps.reshape((-1, 2) + maps.shape[1:])[:, 0]
    left_add = adds.reshape((-1, 2) + adds.shape[1:])[:, 0]
    if state is None:
        size = maps.shape[-1]
        excl_map = jnp.eye(size, dtype=jnp.float32)[None]
        excl_add = jnp.zeros_like(left_add[:1])
        odd_map, odd_add = left_map, left_add
    else:
        excl_map, excl_add = state
        odd_map = jnp.einsum("tij,tjk->tik", excl_map, left_map, precision=HIGHEST)
        odd_add = jnp.einsum("tbj,tjk->tbk", excl_add, left_map, precision=HIGHEST) + left_add
    return interleave(excl_map, odd_map), interleave(excl_add, odd_add)


def down_steps(state, step_adds, even_scale, weights):
    excl_map, excl_add = state
    odd_map = step_right(excl_map, even_scale, weights)
    odd_add = step_right(excl_add, even_scale, weights) + step_adds[0::2]
    return interleave(excl_map, odd_map), interleave(excl_add, odd_add)


def interleave(even, odd):
    return jnp.stack([even, odd], 1).reshape((-1,) + even.shape[1:])


def partner(i, bit):
    if bit >= 4 and (bit.bit_length() - 1) % 2 == 0:
        low = bit // 2
        position = (i // low) % 4
        return i + (3 - 2 * position) * low
    return i ^ bit


def exchanged(x, bit):
    count = lax.axis_size("tm")
    return lax.ppermute(x, "tm", [(i, partner(i, bit)) for i in range(count)])


def batched(lhs, rhs):
    return jnp.einsum("kij,kjl->kil", jnp.stack(lhs), jnp.stack(rhs), precision=HIGHEST)


def local(observations, decay, transition, obs_map, noise_precision, smoother_gain):
    size = transition.shape[0]
    count = lax.axis_size("tm")
    index = lax.axis_index("tm")
    gain_rows = obs_map * noise_precision[:, None]
    closed_rows = transition.T - dot(transition.T, dot(obs_map.T, gain_rows))
    forward_adds = jnp.einsum("wyn,nx->wyx", observations, gain_rows, precision=HIGHEST)

    following = shifted(decay[:1], -1)
    upcoming = jnp.concatenate([decay[1:], following], 0)
    backward_scale = upcoming[::-1]
    maps = jnp.stack([
        pair_maps(decay[0::2], decay[1::2], closed_rows),
        pair_maps(backward_scale[0::2], backward_scale[1::2], smoother_gain.T),
    ])
    adds = step_right(forward_adds[0::2], decay[1::2], closed_rows) + forward_adds[1::2]
    tree = [(maps, adds)]
    while maps.shape[1] > 1:
        pairs = maps.reshape((2, -1, 2) + maps.shape[2:])
        halves = adds.reshape((-1, 2) + adds.shape[1:])
        adds = (
            jnp.einsum("tbj,tjk->tbk", halves[:, 0], pairs[0, :, 1], precision=HIGHEST)
            + halves[:, 1]
        )
        maps = jnp.einsum("dtij,dtjk->dtik", pairs[:, :, 0], pairs[:, :, 1], precision=HIGHEST)
        tree.append((maps, adds))
    forward_maps = [m[0] for m, _ in tree]
    forward_tree = (forward_maps, [a for _, a in tree])
    backward_maps = [m[1] for m, _ in tree]

    rounds = []
    bit = 1
    while bit < count:
        rounds.append(bit)
        bit *= 2
    eye = jnp.eye(size, dtype=jnp.float32)
    total_map, total_add, before_map, before_add = maps[0, 0], adds[0], eye, jnp.zeros_like(adds[0])
    back_total, back_before = maps[1, 0], eye
    stored = []
    sweep = [
        (forward_tree[0][j], forward_tree[1][j])
        for j in reversed(range(len(forward_tree[0]) - 1))
    ]
    state = None
    for k, bit in enumerate(rounds):
        upper = (index & bit) != 0
        if k == len(rounds) - 1:
            got_add = exchanged(total_add, bit)
            entering = jnp.where(upper, dot(got_add, before_map) + before_add, before_add)
            stored.append((back_total, back_total, back_before))
            break
        message = jnp.concatenate([total_map, total_add, back_total], 0)
        if 1 <= k <= len(sweep):
            (state, level), message = lax.optimization_barrier(((state, sweep[k - 1]), message))
            state = down_level(state, *level)
        elif k == len(sweep) + 1:
            state, message = lax.optimization_barrier((state, message))
            state = down_steps(state, forward_adds, decay[0::2], closed_rows)
        got = exchanged(message, bit)
        got_map, got_add, got_back = got[:size], got[size:-size], got[-size:]
        first_map = jnp.where(upper, got_map, total_map)
        second_map = jnp.where(upper, total_map, got_map)
        first_add = jnp.where(upper, got_add, total_add)
        second_add = jnp.where(upper, total_add, got_add)
        back_first = jnp.where(upper, back_total, got_back)
        back_second = jnp.where(upper, got_back, back_total)
        stored.append((back_total, back_second, back_before))
        products = batched(
            [first_map, got_map, back_first, got_back],
            [second_map, before_map, back_second, back_before],
        )
        offsets = batched([first_add, got_add], [second_map, before_map])
        total_map, total_add = products[0], offsets[0] + second_add
        before_map = jnp.where(upper, products[1], before_map)
        before_add = jnp.where(upper, offsets[1] + before_add, before_add)
        back_total = products[2]
        back_before = jnp.where(upper, back_before, products[3])

    for level in sweep[max(0, len(rounds) - 2):]:
        state = down_level(state, *level)
    if len(sweep) + 1 > len(rounds) - 2:
        state = down_steps(state, forward_adds, decay[0::2], closed_rows)
    excl_maps, excl_adds = state
    previous = jnp.einsum("bs,tsr->tbr", entering, excl_maps, precision=HIGHEST) + excl_adds
    filtered = (
        jnp.einsum("tbs,sr->tbr", previous * decay[:, None, :], closed_rows, precision=HIGHEST)
        + forward_adds
    )
    predicted = jnp.einsum(
        "tbs,sr->tbr", filtered * upcoming[:, None, :], transition.T, precision=HIGHEST
    )
    backward_adds = filtered - jnp.einsum(
        "tbs,sr->tbr", predicted * upcoming[:, None, :], smoother_gain.T, precision=HIGHEST
    )
    back_adds = up_sweep_adds(backward_maps, backward_adds[::-1], backward_scale[1::2], smoother_gain.T)

    total_add = back_adds[-1][0]
    before_add = jnp.zeros_like(total_add)
    late_b = (backward_maps, back_adds)
    for k, bit in enumerate(rounds):
        upper = (index & bit) != 0
        own_map, second_map, own_before = stored[k]
        got_add = exchanged(total_add, bit)
        if k == 0:
            late_b, got_add = lax.optimization_barrier((late_b, got_add))
        if k == len(rounds) - 1:
            before_add = jnp.where(upper, before_add, dot(got_add, own_before) + before_add)
            break
        first_add = jnp.where(upper, total_add, got_add)
        second_add = jnp.where(upper, got_add, total_add)
        offsets = batched([first_add, got_add], [second_map, own_before])
        total_add = offsets[0] + second_add
        before_add = jnp.where(upper, before_add, offsets[1] + before_add)
    arriving = before_add
    back_excl_maps = down_sweep_maps(late_b[0], backward_scale[0::2], smoother_gain.T)
    back_excl_adds = down_sweep_adds(
        late_b[0], late_b[1][1:], late_b[1][0], backward_scale[0::2], smoother_gain.T
    )
    following_state = (
        jnp.einsum("bs,tsr->tbr", arriving, back_excl_maps, precision=HIGHEST) + back_excl_adds
    )[::-1]
    smoothed = (
        jnp.einsum(
            "tbs,sr->tbr", following_state * upcoming[:, None, :], smoother_gain.T, precision=HIGHEST
        )
        + backward_adds
    )
    return filtered, smoothed


def solution(mesh):
    in_specs = (P("tm", None, None), P("tm", None), P(), P(), P(), P())
    out_specs = (P("tm", None, None), P("tm", None, None))
    return jax.shard_map(local, mesh=mesh, in_specs=in_specs, out_specs=out_specs, check_vma=False)
```

```python
import jax
import jax.numpy as jnp
from jax import lax
from jax.sharding import PartitionSpec as P

HIGHEST = lax.Precision.HIGHEST


def dot(a, b):
    return jnp.dot(a, b, precision=HIGHEST)


def shifted(x, by):
    count = lax.axis_size("tm")
    pairs = [(i, i + by) for i in range(count) if 0 <= i + by < count]
    return lax.ppermute(x, "tm", pairs)


def step_right(x, scale, weights):
    return jnp.einsum("tbs,sr->tbr", x * scale[:, None, :], weights, precision=HIGHEST)


def pair_maps(first_scale, second_scale, weights):
    scaled = weights[None] * second_scale[:, None, :]
    product = jnp.einsum("tij,jk->tik", scaled, weights, precision=HIGHEST)
    return first_scale[:, :, None] * product


def down_sweep_maps(maps_levels, even_scale, weights):
    size = weights.shape[0]
    eye = jnp.eye(size, dtype=jnp.float32)[None]
    excl = None
    for maps in reversed(maps_levels[:-1]):
        left = maps.reshape((-1, 2) + maps.shape[1:])[:, 0]
        if excl is None:
            excl, odd = eye, left
        else:
            odd = jnp.einsum("tij,tjk->tik", excl, left, precision=HIGHEST)
        excl = interleave(excl, odd)
    if excl is None:
        excl = eye
    return interleave(excl, step_right(excl, even_scale, weights))


def down_sweep_adds(maps_levels, adds_levels, step_adds, even_scale, weights):
    excl = None
    for maps, adds in zip(reversed(maps_levels[:-1]), reversed(adds_levels[:-1])):
        left_map = maps.reshape((-1, 2) + maps.shape[1:])[:, 0]
        left_add = adds.reshape((-1, 2) + adds.shape[1:])[:, 0]
        if excl is None:
            excl, odd = jnp.zeros_like(left_add[:1]), left_add
        else:
            odd = jnp.einsum("tbj,tjk->tbk", excl, left_map, precision=HIGHEST) + left_add
        excl = interleave(excl, odd)
    if excl is None:
        excl = jnp.zeros_like(step_adds[:1])
    return interleave(excl, step_right(excl, even_scale, weights) + step_adds[0::2])


def up_sweep_adds(maps_levels, step_adds, odd_scale, weights):
    adds = step_right(step_adds[0::2], odd_scale, weights) + step_adds[1::2]
    out = [step_adds, adds]
    for maps in maps_levels[:-1]:
        pairs = maps.reshape((-1, 2) + maps.shape[1:])
        halves = adds.reshape((-1, 2) + adds.shape[1:])
        adds = (
            jnp.einsum("tbj,tjk->tbk", halves[:, 0], pairs[:, 1], precision=HIGHEST)
            + halves[:, 1]
        )
        out.append(adds)
    return out


def down_level(state, maps, adds):
    left_map = maps.reshape((-1, 2) + maps.shape[1:])[:, 0]
    left_add = adds.reshape((-1, 2) + adds.shape[1:])[:, 0]
    if state is None:
        size = maps.shape[-1]
        excl_map = jnp.eye(size, dtype=jnp.float32)[None]
        excl_add = jnp.zeros_like(left_add[:1])
        odd_map, odd_add = left_map, left_add
    else:
        excl_map, excl_add = state
        odd_map = jnp.einsum("tij,tjk->tik", excl_map, left_map, precision=HIGHEST)
        odd_add = jnp.einsum("tbj,tjk->tbk", excl_add, left_map, precision=HIGHEST) + left_add
    return interleave(excl_map, odd_map), interleave(excl_add, odd_add)


def down_steps(state, step_adds, even_scale, weights):
    excl_map, excl_add = state
    odd_map = step_right(excl_map, even_scale, weights)
    odd_add = step_right(excl_add, even_scale, weights) + step_adds[0::2]
    return interleave(excl_map, odd_map), interleave(excl_add, odd_add)


def interleave(even, odd):
    return jnp.stack([even, odd], 1).reshape((-1,) + even.shape[1:])


def partner(i, bit):
    if bit >= 4 and (bit.bit_length() - 1) % 2 == 0:
        low = bit // 2
        position = (i // low) % 4
        return i + (3 - 2 * position) * low
    return i ^ bit


def exchanged(x, bit):
    count = lax.axis_size("tm")
    return lax.ppermute(x, "tm", [(i, partner(i, bit)) for i in range(count)])


def batched(lhs, rhs):
    return jnp.einsum("kij,kjl->kil", jnp.stack(lhs), jnp.stack(rhs), precision=HIGHEST)


def local(observations, decay, transition, obs_map, noise_precision, smoother_gain):
    size = transition.shape[0]
    count = lax.axis_size("tm")
    index = lax.axis_index("tm")
    gain_rows = obs_map * noise_precision[:, None]
    closed_rows = transition.T - dot(transition.T, dot(obs_map.T, gain_rows))
    forward_adds = jnp.einsum("wyn,nx->wyx", observations, gain_rows, precision=HIGHEST)

    following = shifted(decay[:1], -1)
    upcoming = jnp.concatenate([decay[1:], following], 0)
    backward_scale = upcoming[::-1]
    maps = jnp.stack([
        pair_maps(decay[0::2], decay[1::2], closed_rows),
        pair_maps(backward_scale[0::2], backward_scale[1::2], smoother_gain.T),
    ])
    adds = step_right(forward_adds[0::2], decay[1::2], closed_rows) + forward_adds[1::2]
    tree = [(maps, adds)]
    while maps.shape[1] > 1:
        pairs = maps.reshape((2, -1, 2) + maps.shape[2:])
        halves = adds.reshape((-1, 2) + adds.shape[1:])
        adds = (
            jnp.einsum("tbj,tjk->tbk", halves[:, 0], pairs[0, :, 1], precision=HIGHEST)
            + halves[:, 1]
        )
        maps = jnp.einsum("dtij,dtjk->dtik", pairs[:, :, 0], pairs[:, :, 1], precision=HIGHEST)
        tree.append((maps, adds))
    forward_maps = [m[0] for m, _ in tree]
    forward_tree = (forward_maps, [a for _, a in tree])
    backward_maps = [m[1] for m, _ in tree]

    rounds = []
    bit = 1
    while bit < count:
        rounds.append(bit)
        bit *= 2
    eye = jnp.eye(size, dtype=jnp.float32)
    total_map, total_add, before_map, before_add = maps[0, 0], adds[0], eye, jnp.zeros_like(adds[0])
    back_total, back_before = maps[1, 0], eye
    stored = []
    sweep = [
        (forward_tree[0][j], forward_tree[1][j])
        for j in reversed(range(len(forward_tree[0]) - 1))
    ]
    state = None
    for k, bit in enumerate(rounds):
        upper = (index & bit) != 0
        if k == len(rounds) - 1:
            got_add = exchanged(total_add, bit)
            entering = jnp.where(upper, dot(got_add, before_map) + before_add, before_add)
            stored.append((back_total, back_total, back_before))
            break
        message = jnp.concatenate([total_map, total_add, back_total], 0)
        if 1 <= k <= len(sweep):
            (state, level), message = lax.optimization_barrier(((state, sweep[k - 1]), message))
            state = down_level(state, *level)
        elif k == len(sweep) + 1:
            state, message = lax.optimization_barrier((state, message))
            state = down_steps(state, forward_adds, decay[0::2], closed_rows)
        got = exchanged(message, bit)
        got_map, got_add, got_back = got[:size], got[size:-size], got[-size:]
        first_map = jnp.where(upper, got_map, total_map)
        second_map = jnp.where(upper, total_map, got_map)
        first_add = jnp.where(upper, got_add, total_add)
        second_add = jnp.where(upper, total_add, got_add)
        back_first = jnp.where(upper, back_total, got_back)
        back_second = jnp.where(upper, got_back, back_total)
        stored.append((back_total, back_second, back_before))
        products = batched(
            [first_map, got_map, back_first, got_back],
            [second_map, before_map, back_second, back_before],
        )
        offsets = batched([first_add, got_add], [second_map, before_map])
        total_map, total_add = products[0], offsets[0] + second_add
        before_map = jnp.where(upper, products[1], before_map)
        before_add = jnp.where(upper, offsets[1] + before_add, before_add)
        back_total = products[2]
        back_before = jnp.where(upper, back_before, products[3])

    for level in sweep[max(0, len(rounds) - 2):]:
        state = down_level(state, *level)
    if len(sweep) + 1 > len(rounds) - 2:
        state = down_steps(state, forward_adds, decay[0::2], closed_rows)
    excl_maps, excl_adds = state
    previous = jnp.einsum("bs,tsr->tbr", entering, excl_maps, precision=HIGHEST) + excl_adds
    filtered = (
        jnp.einsum("tbs,sr->tbr", previous * decay[:, None, :], closed_rows, precision=HIGHEST)
        + forward_adds
    )
    predicted = jnp.einsum(
        "tbs,sr->tbr", filtered * upcoming[:, None, :], transition.T, precision=HIGHEST
    )
    backward_adds = filtered - jnp.einsum(
        "tbs,sr->tbr", predicted * upcoming[:, None, :], smoother_gain.T, precision=HIGHEST
    )
    back_adds = up_sweep_adds(backward_maps, backward_adds[::-1], backward_scale[1::2], smoother_gain.T)

    total_add = back_adds[-1][0]
    before_add = jnp.zeros_like(total_add)
    back_sweep = [
        (backward_maps[j], back_adds[j + 1]) for j in reversed(range(len(backward_maps) - 1))
    ]
    back_state = None
    for k, bit in enumerate(rounds):
        upper = (index & bit) != 0
        own_map, second_map, own_before = stored[k]
        if 1 <= k <= len(back_sweep):
            (back_state, level), total_add = lax.optimization_barrier(
                ((back_state, back_sweep[k - 1]), total_add)
            )
            back_state = down_level(back_state, *level)
        elif k == len(back_sweep) + 1:
            back_state, total_add = lax.optimization_barrier((back_state, total_add))
            back_state = down_steps(back_state, back_adds[0], backward_scale[0::2], smoother_gain.T)
        got_add = exchanged(total_add, bit)
        if k == len(rounds) - 1:
            before_add = jnp.where(upper, before_add, dot(got_add, own_before) + before_add)
            break
        first_add = jnp.where(upper, total_add, got_add)
        second_add = jnp.where(upper, got_add, total_add)
        offsets = batched([first_add, got_add], [second_map, own_before])
        total_add = offsets[0] + second_add
        before_add = jnp.where(upper, before_add, offsets[1] + before_add)
    arriving = before_add
    done = min(len(back_sweep), len(rounds) - 1)
    for level in back_sweep[done:]:
        back_state = down_level(back_state, *level)
    if len(back_sweep) + 1 > len(rounds) - 1:
        back_state = down_steps(back_state, back_adds[0], backward_scale[0::2], smoother_gain.T)
    back_excl_maps, back_excl_adds = back_state
    following_state = (
        jnp.einsum("bs,tsr->tbr", arriving, back_excl_maps, precision=HIGHEST) + back_excl_adds
    )[::-1]
    smoothed = (
        jnp.einsum(
            "tbs,sr->tbr", following_state * upcoming[:, None, :], smoother_gain.T, precision=HIGHEST
        )
        + backward_adds
    )
    return filtered, smoothed


def solution(mesh):
    in_specs = (P("tm", None, None), P("tm", None), P(), P(), P(), P())
    out_specs = (P("tm", None, None), P("tm", None, None))
    return jax.shard_map(local, mesh=mesh, in_specs=in_specs, out_specs=out_specs, check_vma=False)
```

```python
import jax
import jax.numpy as jnp
from jax import lax
from jax.sharding import PartitionSpec as P

HIGHEST = lax.Precision.HIGHEST


def dot(a, b):
    return jnp.dot(a, b, precision=HIGHEST)


def shifted(x, by):
    count = lax.axis_size("tm")
    pairs = [(i, i + by) for i in range(count) if 0 <= i + by < count]
    return lax.ppermute(x, "tm", pairs)


def step_right(x, scale, weights):
    return jnp.einsum("tbs,sr->tbr", x * scale[:, None, :], weights, precision=HIGHEST)


def pair_maps(first_scale, second_scale, weights):
    scaled = weights[None] * second_scale[:, None, :]
    product = jnp.einsum("tij,jk->tik", scaled, weights, precision=HIGHEST)
    return first_scale[:, :, None] * product


def down_sweep_maps(maps_levels, even_scale, weights):
    size = weights.shape[0]
    eye = jnp.eye(size, dtype=jnp.float32)[None]
    excl = None
    for maps in reversed(maps_levels[:-1]):
        left = maps.reshape((-1, 2) + maps.shape[1:])[:, 0]
        if excl is None:
            excl, odd = eye, left
        else:
            odd = jnp.einsum("tij,tjk->tik", excl, left, precision=HIGHEST)
        excl = interleave(excl, odd)
    if excl is None:
        excl = eye
    return interleave(excl, step_right(excl, even_scale, weights))


def down_sweep_adds(maps_levels, adds_levels, step_adds, even_scale, weights):
    excl = None
    for maps, adds in zip(reversed(maps_levels[:-1]), reversed(adds_levels[:-1])):
        left_map = maps.reshape((-1, 2) + maps.shape[1:])[:, 0]
        left_add = adds.reshape((-1, 2) + adds.shape[1:])[:, 0]
        if excl is None:
            excl, odd = jnp.zeros_like(left_add[:1]), left_add
        else:
            odd = jnp.einsum("tbj,tjk->tbk", excl, left_map, precision=HIGHEST) + left_add
        excl = interleave(excl, odd)
    if excl is None:
        excl = jnp.zeros_like(step_adds[:1])
    return interleave(excl, step_right(excl, even_scale, weights) + step_adds[0::2])


def up_sweep_adds(maps_levels, step_adds, odd_scale, weights):
    adds = step_right(step_adds[0::2], odd_scale, weights) + step_adds[1::2]
    out = [step_adds, adds]
    for maps in maps_levels[:-1]:
        pairs = maps.reshape((-1, 2) + maps.shape[1:])
        halves = adds.reshape((-1, 2) + adds.shape[1:])
        adds = (
            jnp.einsum("tbj,tjk->tbk", halves[:, 0], pairs[:, 1], precision=HIGHEST)
            + halves[:, 1]
        )
        out.append(adds)
    return out


def down_level(state, maps, adds):
    left_map = maps.reshape((-1, 2) + maps.shape[1:])[:, 0]
    left_add = adds.reshape((-1, 2) + adds.shape[1:])[:, 0]
    if state is None:
        size = maps.shape[-1]
        excl_map = jnp.eye(size, dtype=jnp.float32)[None]
        excl_add = jnp.zeros_like(left_add[:1])
        odd_map, odd_add = left_map, left_add
    else:
        excl_map, excl_add = state
        odd_map = jnp.einsum("tij,tjk->tik", excl_map, left_map, precision=HIGHEST)
        odd_add = jnp.einsum("tbj,tjk->tbk", excl_add, left_map, precision=HIGHEST) + left_add
    return interleave(excl_map, odd_map), interleave(excl_add, odd_add)


def down_steps(state, step_adds, even_scale, weights):
    excl_map, excl_add = state
    odd_map = step_right(excl_map, even_scale, weights)
    odd_add = step_right(excl_add, even_scale, weights) + step_adds[0::2]
    return interleave(excl_map, odd_map), interleave(excl_add, odd_add)


def interleave(even, odd):
    return jnp.stack([even, odd], 1).reshape((-1,) + even.shape[1:])


def partner(i, bit):
    if bit >= 4 and (bit.bit_length() - 1) % 2 == 0:
        low = bit // 2
        position = (i // low) % 4
        return i + (3 - 2 * position) * low
    return i ^ bit


def exchanged(x, bit):
    count = lax.axis_size("tm")
    return lax.ppermute(x, "tm", [(i, partner(i, bit)) for i in range(count)])


def batched(lhs, rhs):
    return jnp.einsum("kij,kjl->kil", jnp.stack(lhs), jnp.stack(rhs), precision=HIGHEST)


def local(observations, decay, transition, obs_map, noise_precision, smoother_gain):
    size = transition.shape[0]
    count = lax.axis_size("tm")
    index = lax.axis_index("tm")
    gain_rows = obs_map * noise_precision[:, None]
    closed_rows = transition.T - dot(transition.T, dot(obs_map.T, gain_rows))
    forward_adds = jnp.einsum("wyn,nx->wyx", observations, gain_rows, precision=HIGHEST)

    split = jnp.transpose(decay.reshape((-1, 2) + decay.shape[1:]), (1, 0, 2))
    decay_even, decay_odd = split[0], split[1]
    following = shifted(decay_even[:1], -1)
    upcoming = interleave(decay_odd, jnp.concatenate([decay_even[1:], following], 0))
    backward_scale = upcoming[::-1]
    maps = jnp.stack([
        pair_maps(decay_even, decay_odd, closed_rows),
        pair_maps(backward_scale[0::2], backward_scale[1::2], smoother_gain.T),
    ])
    adds = step_right(forward_adds[0::2], decay_odd, closed_rows) + forward_adds[1::2]
    tree = [(maps, adds)]
    while maps.shape[1] > 1:
        pairs = maps.reshape((2, -1, 2) + maps.shape[2:])
        halves = adds.reshape((-1, 2) + adds.shape[1:])
        adds = (
            jnp.einsum("tbj,tjk->tbk", halves[:, 0], pairs[0, :, 1], precision=HIGHEST)
            + halves[:, 1]
        )
        maps = jnp.einsum("dtij,dtjk->dtik", pairs[:, :, 0], pairs[:, :, 1], precision=HIGHEST)
        tree.append((maps, adds))
    forward_maps = [m[0] for m, _ in tree]
    forward_tree = (forward_maps, [a for _, a in tree])
    backward_maps = [m[1] for m, _ in tree]

    rounds = []
    bit = 1
    while bit < count:
        rounds.append(bit)
        bit *= 2
    eye = jnp.eye(size, dtype=jnp.float32)
    total_map, total_add, before_map, before_add = maps[0, 0], adds[0], eye, jnp.zeros_like(adds[0])
    back_total, back_before = maps[1, 0], eye
    stored = []
    sweep = [
        (forward_tree[0][j], forward_tree[1][j])
        for j in reversed(range(len(forward_tree[0]) - 1))
    ]
    state = None
    for k, bit in enumerate(rounds):
        upper = (index & bit) != 0
        if k == len(rounds) - 1:
            got_add = exchanged(total_add, bit)
            entering = jnp.where(upper, dot(got_add, before_map) + before_add, before_add)
            stored.append((back_total, back_total, back_before))
            break
        message = jnp.concatenate([total_map, total_add, back_total], 0)
        if 1 <= k <= len(sweep):
            (state, level), message = lax.optimization_barrier(((state, sweep[k - 1]), message))
            state = down_level(state, *level)
        elif k == len(sweep) + 1:
            state, message = lax.optimization_barrier((state, message))
            state = down_steps(state, forward_adds, decay_even, closed_rows)
        got = exchanged(message, bit)
        got_map, got_add, got_back = got[:size], got[size:-size], got[-size:]
        first_map = jnp.where(upper, got_map, total_map)
        second_map = jnp.where(upper, total_map, got_map)
        first_add = jnp.where(upper, got_add, total_add)
        second_add = jnp.where(upper, total_add, got_add)
        back_first = jnp.where(upper, back_total, got_back)
        back_second = jnp.where(upper, got_back, back_total)
        stored.append((back_total, back_second, back_before))
        products = batched(
            [first_map, got_map, back_first, got_back],
            [second_map, before_map, back_second, back_before],
        )
        offsets = batched([first_add, got_add], [second_map, before_map])
        total_map, total_add = products[0], offsets[0] + second_add
        before_map = jnp.where(upper, products[1], before_map)
        before_add = jnp.where(upper, offsets[1] + before_add, before_add)
        back_total = products[2]
        back_before = jnp.where(upper, back_before, products[3])

    for level in sweep[max(0, len(rounds) - 2):]:
        state = down_level(state, *level)
    if len(sweep) + 1 > len(rounds) - 2:
        state = down_steps(state, forward_adds, decay_even, closed_rows)
    excl_maps, excl_adds = state
    previous = jnp.einsum("bs,tsr->tbr", entering, excl_maps, precision=HIGHEST) + excl_adds
    filtered = (
        jnp.einsum("tbs,sr->tbr", previous * decay[:, None, :], closed_rows, precision=HIGHEST)
        + forward_adds
    )
    predicted = jnp.einsum(
        "tbs,sr->tbr", filtered * upcoming[:, None, :], transition.T, precision=HIGHEST
    )
    backward_adds = filtered - jnp.einsum(
        "tbs,sr->tbr", predicted * upcoming[:, None, :], smoother_gain.T, precision=HIGHEST
    )
    back_adds = up_sweep_adds(backward_maps, backward_adds[::-1], backward_scale[1::2], smoother_gain.T)

    total_add = back_adds[-1][0]
    before_add = jnp.zeros_like(total_add)
    late_b = (backward_maps, back_adds)
    for k, bit in enumerate(rounds):
        upper = (index & bit) != 0
        own_map, second_map, own_before = stored[k]
        got_add = exchanged(total_add, bit)
        if k == 0:
            late_b, got_add = lax.optimization_barrier((late_b, got_add))
        if k == len(rounds) - 1:
            before_add = jnp.where(upper, before_add, dot(got_add, own_before) + before_add)
            break
        first_add = jnp.where(upper, total_add, got_add)
        second_add = jnp.where(upper, got_add, total_add)
        offsets = batched([first_add, got_add], [second_map, own_before])
        total_add = offsets[0] + second_add
        before_add = jnp.where(upper, before_add, offsets[1] + before_add)
    arriving = before_add
    back_excl_maps = down_sweep_maps(late_b[0], backward_scale[0::2], smoother_gain.T)
    back_excl_adds = down_sweep_adds(
        late_b[0], late_b[1][1:], late_b[1][0], backward_scale[0::2], smoother_gain.T
    )
    following_state = (
        jnp.einsum("bs,tsr->tbr", arriving, back_excl_maps, precision=HIGHEST) + back_excl_adds
    )[::-1]
    smoothed = (
        jnp.einsum(
            "tbs,sr->tbr", following_state * upcoming[:, None, :], smoother_gain.T, precision=HIGHEST
        )
        + backward_adds
    )
    return filtered, smoothed


def solution(mesh):
    in_specs = (P("tm", None, None), P("tm", None), P(), P(), P(), P())
    out_specs = (P("tm", None, None), P("tm", None, None))
    return jax.shard_map(local, mesh=mesh, in_specs=in_specs, out_specs=out_specs, check_vma=False)
```

```python
import jax
import jax.numpy as jnp
from jax import lax
from jax.sharding import PartitionSpec as P

HIGHEST = lax.Precision.HIGHEST


def dot(a, b):
    return jnp.dot(a, b, precision=HIGHEST)


def shifted(x, by):
    count = lax.axis_size("tm")
    pairs = [(i, i + by) for i in range(count) if 0 <= i + by < count]
    return lax.ppermute(x, "tm", pairs)


def step_right(x, scale, weights):
    return jnp.einsum("tbs,sr->tbr", x * scale[:, None, :], weights, precision=HIGHEST)


def pair_maps(first_scale, second_scale, weights):
    scaled = weights[None] * second_scale[:, None, :]
    product = jnp.einsum("tij,jk->tik", scaled, weights, precision=HIGHEST)
    return first_scale[:, :, None] * product


def down_sweep_maps(maps_levels, even_scale, weights):
    size = weights.shape[0]
    eye = jnp.eye(size, dtype=jnp.float32)[None]
    excl = None
    for maps in reversed(maps_levels[:-1]):
        left = maps.reshape((-1, 2) + maps.shape[1:])[:, 0]
        if excl is None:
            excl, odd = eye, left
        else:
            odd = jnp.einsum("tij,tjk->tik", excl, left, precision=HIGHEST)
        excl = interleave(excl, odd)
    if excl is None:
        excl = eye
    return interleave(excl, step_right(excl, even_scale, weights))


def down_sweep_adds(maps_levels, adds_levels, step_adds, even_scale, weights):
    excl = None
    for maps, adds in zip(reversed(maps_levels[:-1]), reversed(adds_levels[:-1])):
        left_map = maps.reshape((-1, 2) + maps.shape[1:])[:, 0]
        left_add = adds.reshape((-1, 2) + adds.shape[1:])[:, 0]
        if excl is None:
            excl, odd = jnp.zeros_like(left_add[:1]), left_add
        else:
            odd = jnp.einsum("tbj,tjk->tbk", excl, left_map, precision=HIGHEST) + left_add
        excl = interleave(excl, odd)
    if excl is None:
        excl = jnp.zeros_like(step_adds[:1])
    return interleave(excl, step_right(excl, even_scale, weights) + step_adds[0::2])


def up_sweep_adds(maps_levels, step_adds, odd_scale, weights):
    adds = step_right(step_adds[0::2], odd_scale, weights) + step_adds[1::2]
    out = [step_adds, adds]
    for maps in maps_levels[:-1]:
        pairs = maps.reshape((-1, 2) + maps.shape[1:])
        halves = adds.reshape((-1, 2) + adds.shape[1:])
        adds = (
            jnp.einsum("tbj,tjk->tbk", halves[:, 0], pairs[:, 1], precision=HIGHEST)
            + halves[:, 1]
        )
        out.append(adds)
    return out


def down_level(state, maps, adds):
    left_map = maps.reshape((-1, 2) + maps.shape[1:])[:, 0]
    left_add = adds.reshape((-1, 2) + adds.shape[1:])[:, 0]
    if state is None:
        size = maps.shape[-1]
        excl_map = jnp.eye(size, dtype=jnp.float32)[None]
        excl_add = jnp.zeros_like(left_add[:1])
        odd_map, odd_add = left_map, left_add
    else:
        excl_map, excl_add = state
        odd_map = jnp.einsum("tij,tjk->tik", excl_map, left_map, precision=HIGHEST)
        odd_add = jnp.einsum("tbj,tjk->tbk", excl_add, left_map, precision=HIGHEST) + left_add
    return interleave(excl_map, odd_map), interleave(excl_add, odd_add)


def down_steps(state, step_adds, even_scale, weights):
    excl_map, excl_add = state
    odd_map = step_right(excl_map, even_scale, weights)
    odd_add = step_right(excl_add, even_scale, weights) + step_adds[0::2]
    return interleave(excl_map, odd_map), interleave(excl_add, odd_add)


def interleave(even, odd):
    return jnp.stack([even, odd], 1).reshape((-1,) + even.shape[1:])


def partner(i, bit):
    if bit >= 4 and (bit.bit_length() - 1) % 2 == 0:
        low = bit // 2
        position = (i // low) % 4
        return i + (3 - 2 * position) * low
    return i ^ bit


def exchanged(x, bit):
    count = lax.axis_size("tm")
    return lax.ppermute(x, "tm", [(i, partner(i, bit)) for i in range(count)])


def batched(lhs, rhs):
    return jnp.einsum("kij,kjl->kil", jnp.stack(lhs), jnp.stack(rhs), precision=HIGHEST)


def local(observations, decay, transition, obs_map, noise_precision, smoother_gain):
    size = transition.shape[0]
    count = lax.axis_size("tm")
    index = lax.axis_index("tm")
    gain_rows = obs_map * noise_precision[:, None]
    closed_rows = transition.T - dot(transition.T, dot(obs_map.T, gain_rows))
    forward_adds = jnp.einsum("wyn,nx->wyx", observations, gain_rows, precision=HIGHEST)

    following = shifted(decay[:1], -1)
    upcoming = jnp.concatenate([decay[1:], following], 0)
    backward_scale = upcoming[::-1]
    maps = jnp.stack([
        pair_maps(decay[0::2], decay[1::2], closed_rows),
        pair_maps(backward_scale[0::2], backward_scale[1::2], smoother_gain.T),
    ])
    adds = step_right(forward_adds[0::2], decay[1::2], closed_rows) + forward_adds[1::2]
    tree = [(maps, adds)]
    while maps.shape[1] > 1:
        pairs = maps.reshape((2, -1, 2) + maps.shape[2:])
        halves = adds.reshape((-1, 2) + adds.shape[1:])
        adds = (
            jnp.einsum("tbj,tjk->tbk", halves[:, 0], pairs[0, :, 1], precision=HIGHEST)
            + halves[:, 1]
        )
        maps = jnp.einsum("dtij,dtjk->dtik", pairs[:, :, 0], pairs[:, :, 1], precision=HIGHEST)
        tree.append((maps, adds))
    forward_maps = [m[0] for m, _ in tree]
    forward_tree = (forward_maps, [a for _, a in tree])
    backward_maps = [m[1] for m, _ in tree]

    rounds = []
    bit = 1
    while bit < count:
        rounds.append(bit)
        bit *= 2
    eye = jnp.eye(size, dtype=jnp.float32)
    total_map, total_add, before_map, before_add = maps[0, 0], adds[0], eye, jnp.zeros_like(adds[0])
    back_total, back_before = maps[1, 0], eye
    stored = []
    sweep = [
        (forward_tree[0][j], forward_tree[1][j])
        for j in reversed(range(len(forward_tree[0]) - 1))
    ]
    state = None
    for k, bit in enumerate(rounds):
        upper = (index & bit) != 0
        if k == len(rounds) - 1:
            got_add = exchanged(total_add, bit)
            entering = jnp.where(upper, dot(got_add, before_map) + before_add, before_add)
            stored.append((back_total, back_total, back_before))
            break
        message = jnp.concatenate([total_map, total_add, back_total], 0)
        got = exchanged(message, bit)
        got_map, got_add, got_back = got[:size], got[size:-size], got[-size:]
        first_map = jnp.where(upper, got_map, total_map)
        second_map = jnp.where(upper, total_map, got_map)
        first_add = jnp.where(upper, got_add, total_add)
        second_add = jnp.where(upper, total_add, got_add)
        back_first = jnp.where(upper, back_total, got_back)
        back_second = jnp.where(upper, got_back, back_total)
        stored.append((back_total, back_second, back_before))
        totals = batched([first_map, back_first], [second_map, back_second])
        total_add = dot(first_add, second_map) + second_add
        spans = batched([got_map, got_back], [before_map, back_before])
        if 1 <= k <= len(sweep):
            (state, level), spans = lax.optimization_barrier(((state, sweep[k - 1]), spans))
            state = down_level(state, *level)
        elif k == len(sweep) + 1:
            state, spans = lax.optimization_barrier((state, spans))
            state = down_steps(state, forward_adds, decay[0::2], closed_rows)
        before_add = jnp.where(upper, dot(got_add, before_map) + before_add, before_add)
        total_map, back_total = totals[0], totals[1]
        before_map = jnp.where(upper, spans[0], before_map)
        back_before = jnp.where(upper, back_before, spans[1])

    for level in sweep[max(0, len(rounds) - 2):]:
        state = down_level(state, *level)
    if len(sweep) + 1 > len(rounds) - 2:
        state = down_steps(state, forward_adds, decay[0::2], closed_rows)
    excl_maps, excl_adds = state
    previous = jnp.einsum("bs,tsr->tbr", entering, excl_maps, precision=HIGHEST) + excl_adds
    filtered = (
        jnp.einsum("tbs,sr->tbr", previous * decay[:, None, :], closed_rows, precision=HIGHEST)
        + forward_adds
    )
    predicted = jnp.einsum(
        "tbs,sr->tbr", filtered * upcoming[:, None, :], transition.T, precision=HIGHEST
    )
    backward_adds = filtered - jnp.einsum(
        "tbs,sr->tbr", predicted * upcoming[:, None, :], smoother_gain.T, precision=HIGHEST
    )
    back_adds = up_sweep_adds(backward_maps, backward_adds[::-1], backward_scale[1::2], smoother_gain.T)

    total_add = back_adds[-1][0]
    before_add = jnp.zeros_like(total_add)
    late_b = (backward_maps, back_adds)
    for k, bit in enumerate(rounds):
        upper = (index & bit) != 0
        own_map, second_map, own_before = stored[k]
        got_add = exchanged(total_add, bit)
        if k == 0:
            late_b, got_add = lax.optimization_barrier((late_b, got_add))
        if k == len(rounds) - 1:
            before_add = jnp.where(upper, before_add, dot(got_add, own_before) + before_add)
            break
        first_add = jnp.where(upper, total_add, got_add)
        second_add = jnp.where(upper, got_add, total_add)
        offsets = batched([first_add, got_add], [second_map, own_before])
        total_add = offsets[0] + second_add
        before_add = jnp.where(upper, before_add, offsets[1] + before_add)
    arriving = before_add
    back_excl_maps = down_sweep_maps(late_b[0], backward_scale[0::2], smoother_gain.T)
    back_excl_adds = down_sweep_adds(
        late_b[0], late_b[1][1:], late_b[1][0], backward_scale[0::2], smoother_gain.T
    )
    following_state = (
        jnp.einsum("bs,tsr->tbr", arriving, back_excl_maps, precision=HIGHEST) + back_excl_adds
    )[::-1]
    smoothed = (
        jnp.einsum(
            "tbs,sr->tbr", following_state * upcoming[:, None, :], smoother_gain.T, precision=HIGHEST
        )
        + backward_adds
    )
    return filtered, smoothed


def solution(mesh):
    in_specs = (P("tm", None, None), P("tm", None), P(), P(), P(), P())
    out_specs = (P("tm", None, None), P("tm", None, None))
    return jax.shard_map(local, mesh=mesh, in_specs=in_specs, out_specs=out_specs, check_vma=False)
```

```python
import jax
import jax.numpy as jnp
from jax import lax
from jax.sharding import PartitionSpec as P

HIGHEST = lax.Precision.HIGHEST


def dot(a, b):
    return jnp.dot(a, b, precision=HIGHEST)


def shifted(x, by):
    count = lax.axis_size("tm")
    pairs = [(i, i + by) for i in range(count) if 0 <= i + by < count]
    return lax.ppermute(x, "tm", pairs)


def step_right(x, scale, weights):
    return jnp.einsum("tbs,sr->tbr", x * scale[:, None, :], weights, precision=HIGHEST)


def pair_maps(first_scale, second_scale, weights):
    scaled = weights[None] * second_scale[:, None, :]
    product = jnp.einsum("tij,jk->tik", scaled, weights, precision=HIGHEST)
    return first_scale[:, :, None] * product


def down_sweep_maps(maps_levels, even_scale, weights):
    size = weights.shape[0]
    eye = jnp.eye(size, dtype=jnp.float32)[None]
    excl = None
    for maps in reversed(maps_levels[:-1]):
        left = maps.reshape((-1, 2) + maps.shape[1:])[:, 0]
        if excl is None:
            excl, odd = eye, left
        else:
            odd = jnp.einsum("tij,tjk->tik", excl, left, precision=HIGHEST)
        excl = interleave(excl, odd)
    if excl is None:
        excl = eye
    return interleave(excl, step_right(excl, even_scale, weights))


def down_sweep_adds(maps_levels, adds_levels, step_adds, even_scale, weights):
    excl = None
    for maps, adds in zip(reversed(maps_levels[:-1]), reversed(adds_levels[:-1])):
        left_map = maps.reshape((-1, 2) + maps.shape[1:])[:, 0]
        left_add = adds.reshape((-1, 2) + adds.shape[1:])[:, 0]
        if excl is None:
            excl, odd = jnp.zeros_like(left_add[:1]), left_add
        else:
            odd = jnp.einsum("tbj,tjk->tbk", excl, left_map, precision=HIGHEST) + left_add
        excl = interleave(excl, odd)
    if excl is None:
        excl = jnp.zeros_like(step_adds[:1])
    return interleave(excl, step_right(excl, even_scale, weights) + step_adds[0::2])


def up_sweep_adds(maps_levels, step_adds, odd_scale, weights):
    adds = step_right(step_adds[0::2], odd_scale, weights) + step_adds[1::2]
    out = [step_adds, adds]
    for maps in maps_levels[:-1]:
        pairs = maps.reshape((-1, 2) + maps.shape[1:])
        halves = adds.reshape((-1, 2) + adds.shape[1:])
        adds = (
            jnp.einsum("tbj,tjk->tbk", halves[:, 0], pairs[:, 1], precision=HIGHEST)
            + halves[:, 1]
        )
        out.append(adds)
    return out


def down_level(state, maps, adds):
    left_map = maps.reshape((-1, 2) + maps.shape[1:])[:, 0]
    left_add = adds.reshape((-1, 2) + adds.shape[1:])[:, 0]
    if state is None:
        size = maps.shape[-1]
        excl_map = jnp.eye(size, dtype=jnp.float32)[None]
        excl_add = jnp.zeros_like(left_add[:1])
        odd_map, odd_add = left_map, left_add
    else:
        excl_map, excl_add = state
        odd_map = jnp.einsum("tij,tjk->tik", excl_map, left_map, precision=HIGHEST)
        odd_add = jnp.einsum("tbj,tjk->tbk", excl_add, left_map, precision=HIGHEST) + left_add
    return interleave(excl_map, odd_map), interleave(excl_add, odd_add)


def down_steps(state, step_adds, even_scale, weights):
    excl_map, excl_add = state
    odd_map = step_right(excl_map, even_scale, weights)
    odd_add = step_right(excl_add, even_scale, weights) + step_adds[0::2]
    return interleave(excl_map, odd_map), interleave(excl_add, odd_add)


def interleave(even, odd):
    return jnp.stack([even, odd], 1).reshape((-1,) + even.shape[1:])


def partner(i, bit):
    if bit >= 4 and (bit.bit_length() - 1) % 2 == 0:
        low = bit // 2
        position = (i // low) % 4
        return i + (3 - 2 * position) * low
    return i ^ bit


def exchanged(x, bit):
    count = lax.axis_size("tm")
    return lax.ppermute(x, "tm", [(i, partner(i, bit)) for i in range(count)])


def batched(lhs, rhs):
    return jnp.einsum("kij,kjl->kil", jnp.stack(lhs), jnp.stack(rhs), precision=HIGHEST)


def local(observations, decay, transition, obs_map, noise_precision, smoother_gain):
    size = transition.shape[0]
    count = lax.axis_size("tm")
    index = lax.axis_index("tm")
    gain_rows = obs_map * noise_precision[:, None]
    closed_rows = transition.T - dot(transition.T, dot(obs_map.T, gain_rows))
    forward_adds = jnp.einsum("wyn,nx->wyx", observations, gain_rows, precision=HIGHEST)

    following = shifted(decay[:1], -1)
    upcoming = jnp.concatenate([decay[1:], following], 0)
    backward_scale = upcoming[::-1]
    maps = jnp.stack([
        pair_maps(decay[0::2], decay[1::2], closed_rows),
        pair_maps(backward_scale[0::2], backward_scale[1::2], smoother_gain.T),
    ])
    adds = step_right(forward_adds[0::2], decay[1::2], closed_rows) + forward_adds[1::2]
    tree = [(maps, adds)]
    while maps.shape[1] > 1:
        pairs = maps.reshape((2, -1, 2) + maps.shape[2:])
        halves = adds.reshape((-1, 2) + adds.shape[1:])
        adds = (
            jnp.einsum("tbj,tjk->tbk", halves[:, 0], pairs[0, :, 1], precision=HIGHEST)
            + halves[:, 1]
        )
        maps = jnp.einsum("dtij,dtjk->dtik", pairs[:, :, 0], pairs[:, :, 1], precision=HIGHEST)
        tree.append((maps, adds))
    forward_maps = [m[0] for m, _ in tree]
    forward_tree = (forward_maps, [a for _, a in tree])
    backward_maps = [m[1] for m, _ in tree]

    rounds = []
    bit = 1
    while bit < count:
        rounds.append(bit)
        bit *= 2
    eye = jnp.eye(size, dtype=jnp.float32)
    total_map, total_add, before_map, before_add = maps[0, 0], adds[0], eye, jnp.zeros_like(adds[0])
    back_total, back_before = maps[1, 0], eye
    stored = []
    sweep = [
        (forward_tree[0][j], forward_tree[1][j])
        for j in reversed(range(len(forward_tree[0]) - 1))
    ]
    state = None
    for k, bit in enumerate(rounds):
        upper = (index & bit) != 0
        if k == len(rounds) - 1:
            got_add = exchanged(total_add, bit)
            entering = jnp.where(upper, dot(got_add, before_map) + before_add, before_add)
            stored.append((back_total, back_total, back_before))
            break
        message = jnp.concatenate([total_map, total_add, back_total], 0)
        got = exchanged(message, bit)
        got_map, got_add, got_back = got[:size], got[size:-size], got[-size:]
        first_map = jnp.where(upper, got_map, total_map)
        second_map = jnp.where(upper, total_map, got_map)
        first_add = jnp.where(upper, got_add, total_add)
        second_add = jnp.where(upper, total_add, got_add)
        back_first = jnp.where(upper, back_total, got_back)
        back_second = jnp.where(upper, got_back, back_total)
        stored.append((back_total, back_second, back_before))
        totals = batched([first_map, back_first], [second_map, back_second])
        total_add = dot(first_add, second_map) + second_add
        spans = batched([got_map, got_back], [before_map, back_before])
        if 1 <= k <= len(sweep):
            (state, level), spans = lax.optimization_barrier(((state, sweep[k - 1]), spans))
            state = down_level(state, *level)
        elif k == len(sweep) + 1:
            state, spans = lax.optimization_barrier((state, spans))
            state = down_steps(state, forward_adds, decay[0::2], closed_rows)
        before_add = jnp.where(upper, dot(got_add, before_map) + before_add, before_add)
        total_map, back_total = totals[0], totals[1]
        before_map = jnp.where(upper, spans[0], before_map)
        back_before = jnp.where(upper, back_before, spans[1])

    for level in sweep[max(0, len(rounds) - 2):]:
        state = down_level(state, *level)
    if len(sweep) + 1 > len(rounds) - 2:
        state = down_steps(state, forward_adds, decay[0::2], closed_rows)
    excl_maps, excl_adds = state
    previous = jnp.einsum("bs,tsr->tbr", entering, excl_maps, precision=HIGHEST) + excl_adds
    filtered = (
        jnp.einsum("tbs,sr->tbr", previous * decay[:, None, :], closed_rows, precision=HIGHEST)
        + forward_adds
    )
    predicted = jnp.einsum(
        "tbs,sr->tbr", filtered * upcoming[:, None, :], transition.T, precision=HIGHEST
    )
    backward_adds = filtered - jnp.einsum(
        "tbs,sr->tbr", predicted * upcoming[:, None, :], smoother_gain.T, precision=HIGHEST
    )
    back_adds = up_sweep_adds(backward_maps, backward_adds[::-1], backward_scale[1::2], smoother_gain.T)

    total_add = back_adds[-1][0]
    before_add = jnp.zeros_like(total_add)
    late_b = (backward_maps, back_adds)
    for k, bit in enumerate(rounds):
        upper = (index & bit) != 0
        own_map, second_map, own_before = stored[k]
        got_add = exchanged(total_add, bit)
        if k == 0:
            late_b, got_add = lax.optimization_barrier((late_b, got_add))
        if k == len(rounds) - 1:
            before_add = jnp.where(upper, before_add, dot(got_add, own_before) + before_add)
            break
        first_add = jnp.where(upper, total_add, got_add)
        second_add = jnp.where(upper, got_add, total_add)
        before_add = jnp.where(upper, before_add, dot(got_add, own_before) + before_add)
        total_add = dot(first_add, second_map) + second_add
    arriving = before_add
    back_excl_maps = down_sweep_maps(late_b[0], backward_scale[0::2], smoother_gain.T)
    back_excl_adds = down_sweep_adds(
        late_b[0], late_b[1][1:], late_b[1][0], backward_scale[0::2], smoother_gain.T
    )
    following_state = (
        jnp.einsum("bs,tsr->tbr", arriving, back_excl_maps, precision=HIGHEST) + back_excl_adds
    )[::-1]
    smoothed = (
        jnp.einsum(
            "tbs,sr->tbr", following_state * upcoming[:, None, :], smoother_gain.T, precision=HIGHEST
        )
        + backward_adds
    )
    return filtered, smoothed


def solution(mesh):
    in_specs = (P("tm", None, None), P("tm", None), P(), P(), P(), P())
    out_specs = (P("tm", None, None), P("tm", None, None))
    return jax.shard_map(local, mesh=mesh, in_specs=in_specs, out_specs=out_specs, check_vma=False)
```

```python
import jax
import jax.numpy as jnp
from jax import lax
from jax.sharding import PartitionSpec as P

HIGHEST = lax.Precision.HIGHEST


def dot(a, b):
    return jnp.dot(a, b, precision=HIGHEST)


def shifted(x, by):
    count = lax.axis_size("tm")
    pairs = [(i, i + by) for i in range(count) if 0 <= i + by < count]
    return lax.ppermute(x, "tm", pairs)


def step_right(x, scale, weights):
    return jnp.einsum("tbs,sr->tbr", x * scale[:, None, :], weights, precision=HIGHEST)


def pair_maps(first_scale, second_scale, weights):
    scaled = weights[None] * second_scale[:, None, :]
    product = jnp.einsum("tij,jk->tik", scaled, weights, precision=HIGHEST)
    return first_scale[:, :, None] * product


def down_sweep_maps(maps_levels, even_scale, weights):
    size = weights.shape[0]
    eye = jnp.eye(size, dtype=jnp.float32)[None]
    excl = None
    for maps in reversed(maps_levels[:-1]):
        left = maps.reshape((-1, 2) + maps.shape[1:])[:, 0]
        if excl is None:
            excl, odd = eye, left
        else:
            odd = jnp.einsum("tij,tjk->tik", excl, left, precision=HIGHEST)
        excl = interleave(excl, odd)
    if excl is None:
        excl = eye
    return interleave(excl, step_right(excl, even_scale, weights))


def down_sweep_adds(maps_levels, adds_levels, step_adds, even_scale, weights):
    excl = None
    for maps, adds in zip(reversed(maps_levels[:-1]), reversed(adds_levels[:-1])):
        left_map = maps.reshape((-1, 2) + maps.shape[1:])[:, 0]
        left_add = adds.reshape((-1, 2) + adds.shape[1:])[:, 0]
        if excl is None:
            excl, odd = jnp.zeros_like(left_add[:1]), left_add
        else:
            odd = jnp.einsum("tbj,tjk->tbk", excl, left_map, precision=HIGHEST) + left_add
        excl = interleave(excl, odd)
    if excl is None:
        excl = jnp.zeros_like(step_adds[:1])
    return interleave(excl, step_right(excl, even_scale, weights) + step_adds[0::2])


def up_sweep_adds(maps_levels, step_adds, odd_scale, weights):
    adds = step_right(step_adds[0::2], odd_scale, weights) + step_adds[1::2]
    out = [step_adds, adds]
    for maps in maps_levels[:-1]:
        pairs = maps.reshape((-1, 2) + maps.shape[1:])
        halves = adds.reshape((-1, 2) + adds.shape[1:])
        adds = (
            jnp.einsum("tbj,tjk->tbk", halves[:, 0], pairs[:, 1], precision=HIGHEST)
            + halves[:, 1]
        )
        out.append(adds)
    return out


def down_level(state, maps, adds):
    left_map = maps.reshape((-1, 2) + maps.shape[1:])[:, 0]
    left_add = adds.reshape((-1, 2) + adds.shape[1:])[:, 0]
    if state is None:
        size = maps.shape[-1]
        excl_map = jnp.eye(size, dtype=jnp.float32)[None]
        excl_add = jnp.zeros_like(left_add[:1])
        odd_map, odd_add = left_map, left_add
    else:
        excl_map, excl_add = state
        odd_map = jnp.einsum("tij,tjk->tik", excl_map, left_map, precision=HIGHEST)
        odd_add = jnp.einsum("tbj,tjk->tbk", excl_add, left_map, precision=HIGHEST) + left_add
    return interleave(excl_map, odd_map), interleave(excl_add, odd_add)


def down_steps(state, step_adds, even_scale, weights):
    excl_map, excl_add = state
    odd_map = step_right(excl_map, even_scale, weights)
    odd_add = step_right(excl_add, even_scale, weights) + step_adds[0::2]
    return interleave(excl_map, odd_map), interleave(excl_add, odd_add)


def interleave(even, odd):
    return jnp.stack([even, odd], 1).reshape((-1,) + even.shape[1:])


def partner(i, bit):
    if bit >= 4 and (bit.bit_length() - 1) % 2 == 0:
        low = bit // 2
        position = (i // low) % 4
        return i + (3 - 2 * position) * low
    return i ^ bit


def exchanged(x, bit):
    count = lax.axis_size("tm")
    return lax.ppermute(x, "tm", [(i, partner(i, bit)) for i in range(count)])


def batched(lhs, rhs):
    return jnp.einsum("kij,kjl->kil", jnp.stack(lhs), jnp.stack(rhs), precision=HIGHEST)


def local(observations, decay, transition, obs_map, noise_precision, smoother_gain):
    size = transition.shape[0]
    count = lax.axis_size("tm")
    index = lax.axis_index("tm")
    gain_rows = obs_map * noise_precision[:, None]
    closed_rows = transition.T - dot(transition.T, dot(obs_map.T, gain_rows))
    forward_adds = jnp.einsum("wyn,nx->wyx", observations, gain_rows, precision=HIGHEST)

    following = shifted(decay[:1], -1)
    upcoming = jnp.concatenate([decay[1:], following], 0)
    backward_scale = upcoming[::-1]
    maps = jnp.stack([
        pair_maps(decay[0::2], decay[1::2], closed_rows),
        pair_maps(backward_scale[0::2], backward_scale[1::2], smoother_gain.T),
    ])
    adds = step_right(forward_adds[0::2], decay[1::2], closed_rows) + forward_adds[1::2]
    tree = [(maps, adds)]
    while maps.shape[1] > 1:
        pairs = maps.reshape((2, -1, 2) + maps.shape[2:])
        halves = adds.reshape((-1, 2) + adds.shape[1:])
        adds = (
            jnp.einsum("tbj,tjk->tbk", halves[:, 0], pairs[0, :, 1], precision=HIGHEST)
            + halves[:, 1]
        )
        maps = jnp.einsum("dtij,dtjk->dtik", pairs[:, :, 0], pairs[:, :, 1], precision=HIGHEST)
        tree.append((maps, adds))
    forward_maps = [m[0] for m, _ in tree]
    forward_tree = (forward_maps, [a for _, a in tree])
    backward_maps = [m[1] for m, _ in tree]

    rounds = []
    bit = 1
    while bit < count:
        rounds.append(bit)
        bit *= 2
    eye = jnp.eye(size, dtype=jnp.float32)
    total_map, total_add, before_map, before_add = maps[0, 0], adds[0], eye, jnp.zeros_like(adds[0])
    back_total, back_before = maps[1, 0], eye
    stored = []
    sweep = [
        (forward_tree[0][j], forward_tree[1][j])
        for j in reversed(range(len(forward_tree[0]) - 1))
    ]
    state = None
    for k, bit in enumerate(rounds):
        upper = (index & bit) != 0
        if k == len(rounds) - 1:
            got_add = exchanged(total_add, bit)
            entering = jnp.where(upper, dot(got_add, before_map) + before_add, before_add)
            stored.append((back_total, back_total, back_before))
            break
        message = jnp.concatenate([total_map, total_add, back_total], 0)
        got = exchanged(message, bit)
        got_map, got_add, got_back = got[:size], got[size:-size], got[-size:]
        first_map = jnp.where(upper, got_map, total_map)
        second_map = jnp.where(upper, total_map, got_map)
        first_add = jnp.where(upper, got_add, total_add)
        second_add = jnp.where(upper, total_add, got_add)
        back_first = jnp.where(upper, back_total, got_back)
        back_second = jnp.where(upper, got_back, back_total)
        stored.append((back_total, back_second, back_before))
        totals = batched([first_map, back_first], [second_map, back_second])
        total_add = dot(first_add, second_map) + second_add
        spans = batched([got_map, got_back], [before_map, back_before])
        if k < len(sweep):
            (state, level), spans = lax.optimization_barrier(((state, sweep[k]), spans))
            state = down_level(state, *level)
        elif k == len(sweep):
            state, spans = lax.optimization_barrier((state, spans))
            state = down_steps(state, forward_adds, decay[0::2], closed_rows)
        before_add = jnp.where(upper, dot(got_add, before_map) + before_add, before_add)
        total_map, back_total = totals[0], totals[1]
        before_map = jnp.where(upper, spans[0], before_map)
        back_before = jnp.where(upper, back_before, spans[1])

    for level in sweep[max(0, len(rounds) - 1):]:
        state = down_level(state, *level)
    if len(sweep) > len(rounds) - 2:
        state = down_steps(state, forward_adds, decay[0::2], closed_rows)
    excl_maps, excl_adds = state
    previous = jnp.einsum("bs,tsr->tbr", entering, excl_maps, precision=HIGHEST) + excl_adds
    filtered = (
        jnp.einsum("tbs,sr->tbr", previous * decay[:, None, :], closed_rows, precision=HIGHEST)
        + forward_adds
    )
    predicted = jnp.einsum(
        "tbs,sr->tbr", filtered * upcoming[:, None, :], transition.T, precision=HIGHEST
    )
    backward_adds = filtered - jnp.einsum(
        "tbs,sr->tbr", predicted * upcoming[:, None, :], smoother_gain.T, precision=HIGHEST
    )
    back_adds = up_sweep_adds(backward_maps, backward_adds[::-1], backward_scale[1::2], smoother_gain.T)

    total_add = back_adds[-1][0]
    before_add = jnp.zeros_like(total_add)
    late_b = (backward_maps, back_adds)
    for k, bit in enumerate(rounds):
        upper = (index & bit) != 0
        own_map, second_map, own_before = stored[k]
        got_add = exchanged(total_add, bit)
        if k == 0:
            late_b, got_add = lax.optimization_barrier((late_b, got_add))
        if k == len(rounds) - 1:
            before_add = jnp.where(upper, before_add, dot(got_add, own_before) + before_add)
            break
        first_add = jnp.where(upper, total_add, got_add)
        second_add = jnp.where(upper, got_add, total_add)
        offsets = batched([first_add, got_add], [second_map, own_before])
        total_add = offsets[0] + second_add
        before_add = jnp.where(upper, before_add, offsets[1] + before_add)
    arriving = before_add
    back_excl_maps = down_sweep_maps(late_b[0], backward_scale[0::2], smoother_gain.T)
    back_excl_adds = down_sweep_adds(
        late_b[0], late_b[1][1:], late_b[1][0], backward_scale[0::2], smoother_gain.T
    )
    following_state = (
        jnp.einsum("bs,tsr->tbr", arriving, back_excl_maps, precision=HIGHEST) + back_excl_adds
    )[::-1]
    smoothed = (
        jnp.einsum(
            "tbs,sr->tbr", following_state * upcoming[:, None, :], smoother_gain.T, precision=HIGHEST
        )
        + backward_adds
    )
    return filtered, smoothed


def solution(mesh):
    in_specs = (P("tm", None, None), P("tm", None), P(), P(), P(), P())
    out_specs = (P("tm", None, None), P("tm", None, None))
    return jax.shard_map(local, mesh=mesh, in_specs=in_specs, out_specs=out_specs, check_vma=False)
```

```python
import jax
import jax.numpy as jnp
from jax import lax
from jax.sharding import PartitionSpec as P

HIGHEST = lax.Precision.HIGHEST


def dot(a, b):
    return jnp.dot(a, b, precision=HIGHEST)


def shifted(x, by):
    count = lax.axis_size("tm")
    pairs = [(i, i + by) for i in range(count) if 0 <= i + by < count]
    return lax.ppermute(x, "tm", pairs)


def step_right(x, scale, weights):
    return jnp.einsum("tbs,sr->tbr", x * scale[:, None, :], weights, precision=HIGHEST)


def pair_maps(first_scale, second_scale, weights):
    scaled = weights[None] * second_scale[:, None, :]
    product = jnp.einsum("tij,jk->tik", scaled, weights, precision=HIGHEST)
    return first_scale[:, :, None] * product


def down_sweep_maps(maps_levels, even_scale, weights):
    size = weights.shape[0]
    eye = jnp.eye(size, dtype=jnp.float32)[None]
    excl = None
    for maps in reversed(maps_levels[:-1]):
        left = maps.reshape((-1, 2) + maps.shape[1:])[:, 0]
        if excl is None:
            excl, odd = eye, left
        else:
            odd = jnp.einsum("tij,tjk->tik", excl, left, precision=HIGHEST)
        excl = interleave(excl, odd)
    if excl is None:
        excl = eye
    return interleave(excl, step_right(excl, even_scale, weights))


def down_sweep_adds(maps_levels, adds_levels, step_adds, even_scale, weights):
    excl = None
    for maps, adds in zip(reversed(maps_levels[:-1]), reversed(adds_levels[:-1])):
        left_map = maps.reshape((-1, 2) + maps.shape[1:])[:, 0]
        left_add = adds.reshape((-1, 2) + adds.shape[1:])[:, 0]
        if excl is None:
            excl, odd = jnp.zeros_like(left_add[:1]), left_add
        else:
            odd = jnp.einsum("tbj,tjk->tbk", excl, left_map, precision=HIGHEST) + left_add
        excl = interleave(excl, odd)
    if excl is None:
        excl = jnp.zeros_like(step_adds[:1])
    return interleave(excl, step_right(excl, even_scale, weights) + step_adds[0::2])


def up_sweep_adds(maps_levels, step_adds, odd_scale, weights):
    adds = step_right(step_adds[0::2], odd_scale, weights) + step_adds[1::2]
    out = [step_adds, adds]
    for maps in maps_levels[:-1]:
        pairs = maps.reshape((-1, 2) + maps.shape[1:])
        halves = adds.reshape((-1, 2) + adds.shape[1:])
        adds = (
            jnp.einsum("tbj,tjk->tbk", halves[:, 0], pairs[:, 1], precision=HIGHEST)
            + halves[:, 1]
        )
        out.append(adds)
    return out


def down_level(state, maps, adds):
    left_map = maps.reshape((-1, 2) + maps.shape[1:])[:, 0]
    left_add = adds.reshape((-1, 2) + adds.shape[1:])[:, 0]
    if state is None:
        size = maps.shape[-1]
        excl_map = jnp.eye(size, dtype=jnp.float32)[None]
        excl_add = jnp.zeros_like(left_add[:1])
        odd_map, odd_add = left_map, left_add
    else:
        excl_map, excl_add = state
        odd_map = jnp.einsum("tij,tjk->tik", excl_map, left_map, precision=HIGHEST)
        odd_add = jnp.einsum("tbj,tjk->tbk", excl_add, left_map, precision=HIGHEST) + left_add
    return interleave(excl_map, odd_map), interleave(excl_add, odd_add)


def down_steps(state, step_adds, even_scale, weights):
    excl_map, excl_add = state
    odd_map = step_right(excl_map, even_scale, weights)
    odd_add = step_right(excl_add, even_scale, weights) + step_adds[0::2]
    return interleave(excl_map, odd_map), interleave(excl_add, odd_add)


def interleave(even, odd):
    return jnp.stack([even, odd], 1).reshape((-1,) + even.shape[1:])


def partner(i, bit):
    if bit >= 4 and (bit.bit_length() - 1) % 2 == 0:
        low = bit // 2
        position = (i // low) % 4
        return i + (3 - 2 * position) * low
    return i ^ bit


def exchanged(x, bit):
    count = lax.axis_size("tm")
    return lax.ppermute(x, "tm", [(i, partner(i, bit)) for i in range(count)])


def batched(lhs, rhs):
    return jnp.einsum("kij,kjl->kil", jnp.stack(lhs), jnp.stack(rhs), precision=HIGHEST)


def local(observations, decay, transition, obs_map, noise_precision, smoother_gain):
    size = transition.shape[0]
    count = lax.axis_size("tm")
    index = lax.axis_index("tm")
    gain_rows = obs_map * noise_precision[:, None]
    closed_rows = transition.T - dot(transition.T, dot(obs_map.T, gain_rows))
    forward_adds = jnp.einsum("wyn,nx->wyx", observations, gain_rows, precision=HIGHEST)

    following = shifted(decay[:1], -1)
    upcoming = jnp.concatenate([decay[1:], following], 0)
    backward_scale = upcoming[::-1]
    maps = jnp.stack([
        pair_maps(decay[0::2], decay[1::2], closed_rows),
        pair_maps(backward_scale[0::2], backward_scale[1::2], smoother_gain.T),
    ])
    adds = step_right(forward_adds[0::2], decay[1::2], closed_rows) + forward_adds[1::2]
    tree = [(maps, adds)]
    while maps.shape[1] > 1:
        pairs = maps.reshape((2, -1, 2) + maps.shape[2:])
        halves = adds.reshape((-1, 2) + adds.shape[1:])
        adds = (
            jnp.einsum("tbj,tjk->tbk", halves[:, 0], pairs[0, :, 1], precision=HIGHEST)
            + halves[:, 1]
        )
        maps = jnp.einsum("dtij,dtjk->dtik", pairs[:, :, 0], pairs[:, :, 1], precision=HIGHEST)
        tree.append((maps, adds))
    forward_maps = [m[0] for m, _ in tree]
    forward_tree = (forward_maps, [a for _, a in tree])
    backward_maps = [m[1] for m, _ in tree]

    rounds = []
    bit = 1
    while bit < count:
        rounds.append(bit)
        bit *= 2
    eye = jnp.eye(size, dtype=jnp.float32)
    total_map, total_add, before_map, before_add = maps[0, 0], adds[0], eye, jnp.zeros_like(adds[0])
    back_total, back_before = maps[1, 0], eye
    stored = []
    sweep = [
        (forward_tree[0][j], forward_tree[1][j])
        for j in reversed(range(len(forward_tree[0]) - 1))
    ]
    state = None
    for k, bit in enumerate(rounds):
        upper = (index & bit) != 0
        if k == len(rounds) - 1:
            got_add = exchanged(total_add, bit)
            entering = jnp.where(upper, dot(got_add, before_map) + before_add, before_add)
            stored.append((back_total, back_total, back_before))
            break
        message = jnp.concatenate([total_map, total_add, back_total], 0)
        got = exchanged(message, bit)
        got_map, got_add, got_back = got[:size], got[size:-size], got[-size:]
        first_map = jnp.where(upper, got_map, total_map)
        second_map = jnp.where(upper, total_map, got_map)
        first_add = jnp.where(upper, got_add, total_add)
        second_add = jnp.where(upper, total_add, got_add)
        back_first = jnp.where(upper, back_total, got_back)
        back_second = jnp.where(upper, got_back, back_total)
        stored.append((back_total, back_second, back_before))
        totals = batched([first_map, back_first], [second_map, back_second])
        total_add = dot(first_add, second_map) + second_add
        spans = batched([got_map, got_back], [before_map, back_before])
        if k < len(sweep):
            (state, level), spans = lax.optimization_barrier(((state, sweep[k]), spans))
            state = down_level(state, *level)
        elif k == len(sweep):
            state, spans = lax.optimization_barrier((state, spans))
            state = down_steps(state, forward_adds, decay[0::2], closed_rows)
        before_add = jnp.where(upper, dot(got_add, before_map) + before_add, before_add)
        total_map, back_total = totals[0], totals[1]
        before_map = jnp.where(upper, spans[0], before_map)
        back_before = jnp.where(upper, back_before, spans[1])

    for level in sweep[max(0, len(rounds) - 1):]:
        state = down_level(state, *level)
    if len(sweep) > len(rounds) - 2:
        state = down_steps(state, forward_adds, decay[0::2], closed_rows)
    excl_maps, excl_adds = state
    previous = jnp.einsum("bs,tsr->tbr", entering, excl_maps, precision=HIGHEST) + excl_adds
    filtered = (
        jnp.einsum("tbs,sr->tbr", previous * decay[:, None, :], closed_rows, precision=HIGHEST)
        + forward_adds
    )
    predicted = jnp.einsum(
        "tbs,sr->tbr", filtered * upcoming[:, None, :], transition.T, precision=HIGHEST
    )
    backward_adds = filtered - jnp.einsum(
        "tbs,sr->tbr", predicted * upcoming[:, None, :], smoother_gain.T, precision=HIGHEST
    )
    back_adds = up_sweep_adds(backward_maps, backward_adds[::-1], backward_scale[1::2], smoother_gain.T)

    total_add = back_adds[-1][0]
    before_add = jnp.zeros_like(total_add)
    late_b = (backward_maps, back_adds)
    for k, bit in enumerate(rounds):
        upper = (index & bit) != 0
        own_map, second_map, own_before = stored[k]
        got_add = exchanged(total_add, bit)
        if k == min(1, len(rounds) - 1):
            late_b, got_add = lax.optimization_barrier((late_b, got_add))
        if k == len(rounds) - 1:
            before_add = jnp.where(upper, before_add, dot(got_add, own_before) + before_add)
            break
        first_add = jnp.where(upper, total_add, got_add)
        second_add = jnp.where(upper, got_add, total_add)
        offsets = batched([first_add, got_add], [second_map, own_before])
        total_add = offsets[0] + second_add
        before_add = jnp.where(upper, before_add, offsets[1] + before_add)
    arriving = before_add
    back_excl_maps = down_sweep_maps(late_b[0], backward_scale[0::2], smoother_gain.T)
    back_excl_adds = down_sweep_adds(
        late_b[0], late_b[1][1:], late_b[1][0], backward_scale[0::2], smoother_gain.T
    )
    following_state = (
        jnp.einsum("bs,tsr->tbr", arriving, back_excl_maps, precision=HIGHEST) + back_excl_adds
    )[::-1]
    smoothed = (
        jnp.einsum(
            "tbs,sr->tbr", following_state * upcoming[:, None, :], smoother_gain.T, precision=HIGHEST
        )
        + backward_adds
    )
    return filtered, smoothed


def solution(mesh):
    in_specs = (P("tm", None, None), P("tm", None), P(), P(), P(), P())
    out_specs = (P("tm", None, None), P("tm", None, None))
    return jax.shard_map(local, mesh=mesh, in_specs=in_specs, out_specs=out_specs, check_vma=False)
```
